256 devices in a mesh: seq: 8 (over x, core), dp: 32 (over y, z).
Axes of the slice: x: 4, y: 4, z: 8, core: 2. Of those that a mesh axis runs over, the one named last changes fastest.
Arguments:
- queries: bfloat16 [32, 1024, 4096], P('dp', 'seq'), may hold values from -4.5 to 4.5
- rotated_key_matrix: bfloat16 [32, 1024, 1024], P('dp', 'seq'), may hold values from -4.5 to 4.5
- value_matrix: bfloat16 [32, 1024, 1024], P('dp', 'seq'), may hold values from -6 to 6
- out_weight: bfloat16 [4096, 2048], P('seq'), may hold values from -0.09375 to 0.09375
- out_grad: bfloat16 [32, 1024, 2048], P('dp', 'seq'), may hold values from -6 to 6
- lengths: int32 [32, 16], P('dp'), may hold values from 1 to 256, 1024 in all within a row
- pack_order: int32 [32, 16], P('dp'), may hold values from 0 to 15, each once within a row
Outputs:
- layer_out: bfloat16 [32, 1024, 2048], P('dp', 'seq')
- query_grad: bfloat16 [32, 1024, 4096], P('dp', 'seq')
- key_grad: bfloat16 [32, 1024, 1024], P('dp', 'seq')
- value_grad: bfloat16 [32, 1024, 1024], P('dp', 'seq')
- weight_grad: float32 [4096, 2048], P('seq', 'dp')
The draws below stay inside these ranges and needn't reach their ends.
Inputs may be any that keep to these rules, and one draw needn't show every extreme that they name: The 16 lengths of a window sum to 1024; the longest is 256. `pack_order`: each row names every sample once.
All inputs are finite; a program needn't handle non-finite values.
Results may differ from the reference program's by a relative error of at most 0.017.
Values may be sent and summed in bfloat16 or wider, within the bound.
No kernel may reach another device: no remote copies, remote signals or barrier semaphores. Data moves between devices by JAX's collectives and lax.ppermute only.
A program may use at most 128 MiB of HBM per device.

```python
import math
import jax
import jax.numpy as jnp
import numpy as np
from jax import lax

D = 2048
QUERY_HEADS = 32
KEY_VALUE_HEADS = 8
HEAD_SIZE = 128
NSAMP = 16
WINDOW_TOKENS = 1024
WINDOW_COUNT = 32
MOST = 256
N_SEQ = 8


def draw_queries(key, part):
    return jax.random.truncated_normal(jax.random.fold_in(key, 105), -4.5, 4.5, (WINDOW_COUNT, WINDOW_TOKENS, QUERY_HEADS * HEAD_SIZE), jnp.float32).astype(jnp.bfloat16)


def draw_rotated_key_matrix(key, part):
    return jax.random.truncated_normal(jax.random.fold_in(key, 107), -4.5, 4.5, (WINDOW_COUNT, WINDOW_TOKENS, KEY_VALUE_HEADS * HEAD_SIZE), jnp.float32).astype(jnp.bfloat16)


def with_spikes(drawn, own_key, source, target, blocks, factor):
    owner, partner = [(jnp.arange(drawn.shape[axis_at]) // (drawn.shape[axis_at] // blocks)).reshape([-1 if axis == axis_at else 1 for axis in range(drawn.ndim)]) for axis_at in (source, target)]
    chosen = jax.random.permutation(own_key, blocks)[partner]
    strong = (owner == chosen) | (owner == (partner + blocks // 2) % blocks)
    return jnp.where(strong, factor * drawn, drawn)


def block_scale(stream_key, shape, split, least, top_value):
    factor_of, own = 1.0, jax.random.fold_in(stream_key, 6)
    for dim, blocks in split:
        draws = jnp.exp(jax.random.uniform(jax.random.fold_in(own, dim), (blocks,), jnp.float32, least / len(split), top_value / len(split)))
        factor_of = factor_of * jnp.repeat(draws, shape[dim] // blocks).reshape([-1 if axis == dim else 1 for axis in range(len(shape))])
    return factor_of


def profile(number_of, total, limit, slope):
    loads = [(1 << 20) // math.isqrt(rank ** slope) + 1 for rank in range(2, number_of + 1)]
    spare, counts = total - limit - (number_of - 1), [1] * (number_of - 1)
    while spare > 0:
        candidates = [i for i in range(number_of - 1) if counts[i] < limit]
        mass, budget = sum([loads[i] for i in candidates]), spare
        for i in candidates:
            more = min(limit - counts[i], max(1, budget * loads[i] // mass), spare)
            counts[i] = counts[i] + more
            spare = spare - more
    return np.array([limit] + counts)


def uneven(key, number_of, total, bound, slope):
    if number_of == 2:
        one = jax.random.randint(key, (), max(1, total - bound), min(bound, total - 1) + 1)
        return jnp.stack([one, total - one])
    tallies = jnp.asarray(profile(number_of, total, bound, slope), jnp.int32)
    pairs = (number_of - 1) // 2
    donor, sink = tallies[1:1 + 2 * pairs:2], tallies[2:2 + 2 * pairs:2]
    margin = jnp.minimum(donor - 1, bound - sink)
    shifted = jax.random.randint(jax.random.fold_in(key, 1), (pairs,), 0, 1 << 20) % (margin + 1)
    tallies = tallies.at[1:1 + 2 * pairs:2].set(donor - shifted).at[2:2 + 2 * pairs:2].set(sink + shifted)
    return tallies[jax.random.permutation(jax.random.fold_in(key, 2), number_of)]


def centred(rng, extent, deviation, most, split=(), kind=jnp.bfloat16):
    loudness = block_scale(rng, extent, split, -0.22, 0.18) if split else 1.0
    result = jax.random.normal(rng, extent, jnp.float32) * deviation * loudness
    return jnp.minimum(jnp.maximum(result, -most), most).astype(kind)


def heavy_noise(key, extent, deviation, bound, shards, heavy, kind=jnp.bfloat16):
    entries = deviation * jax.random.normal(key, extent, jnp.float32)
    if shards:
        entries = entries * block_scale(key, extent, shards, -0.22, 0.18)
    return jnp.clip(with_spikes(entries, jax.random.fold_in(key, 3), *heavy), -bound, bound).astype(kind)


def setup_inputs(seed: int = 0) -> dict:
    keys = jax.random.split(jax.random.key(seed), 8)
    queries = draw_queries(jax.random.fold_in(keys[7], 71), 0)
    rotated_key_matrix = draw_rotated_key_matrix(jax.random.fold_in(keys[7], 71), 0)
    value_matrix = centred(keys[2], (WINDOW_COUNT, WINDOW_TOKENS, KEY_VALUE_HEADS * HEAD_SIZE), 1.0, 6.0, ((0, 32), (1, 8)))
    out_weight = centred(keys[3], (QUERY_HEADS * HEAD_SIZE, D), (QUERY_HEADS * HEAD_SIZE) ** -0.5, 0.09375, ((0, 8),))
    out_grad = heavy_noise(keys[4], (WINDOW_COUNT, WINDOW_TOKENS, D), 1.0, 6.0, ((0, 32), (1, 8)), (0, 2, 32, 2.75))
    lengths = jax.vmap(lambda own: uneven(own, NSAMP, WINDOW_TOKENS, MOST, 2))(jax.random.split(keys[5], WINDOW_COUNT)).reshape((WINDOW_COUNT, NSAMP)).astype(jnp.int32)
    pack_order = jax.vmap(lambda own: jax.random.permutation(own, NSAMP))(jax.random.split(keys[6], WINDOW_COUNT)).reshape((WINDOW_COUNT, NSAMP)).astype(jnp.int32)
    return {"queries": queries, "rotated_key_matrix": rotated_key_matrix, "value_matrix": value_matrix, "out_weight": out_weight, "out_grad": out_grad, "lengths": lengths, "pack_order": pack_order}


def row_starts(lengths, pack_order, win_rows):
    samples = lengths.shape[0]
    picked = jnp.sum(jnp.where(pack_order[:, None] == jnp.arange(samples, dtype=jnp.int32)[None, :], lengths[None, :], 0), axis=1, dtype=jnp.int32)
    seg_ends = jnp.cumsum(picked, dtype=jnp.int32)
    places = jnp.arange(win_rows, dtype=jnp.int32)
    return jnp.sum(jnp.where(seg_ends[None, :] <= places[:, None], picked[None, :], 0), axis=1, dtype=jnp.int32)


def reference(queries, rotated_key_matrix, value_matrix, out_weight, out_grad, lengths, pack_order):
    group_width = QUERY_HEADS // KEY_VALUE_HEADS
    head_scale = HEAD_SIZE ** -0.5
    group_cols = QUERY_HEADS * HEAD_SIZE // N_SEQ
    wo_float = out_weight.astype(jnp.float32)
    wo_groups = wo_float.reshape(N_SEQ, group_cols, D)

    def window(wo_grad, window_in):
        query_window, key_window, value_window, g_win, len_win, ord_win = window_in
        starts = row_starts(len_win, ord_win, WINDOW_TOKENS)
        places = jnp.arange(WINDOW_TOKENS, dtype=jnp.int32)
        visible = (places[None, :] >= starts[:, None]) & (places[None, :] <= places[:, None])
        query_head_rows = query_window.reshape(WINDOW_TOKENS, KEY_VALUE_HEADS, group_width, HEAD_SIZE).astype(jnp.float32)
        key_head_rows = key_window.reshape(WINDOW_TOKENS, KEY_VALUE_HEADS, HEAD_SIZE).astype(jnp.float32)
        value_head_rows = value_window.reshape(WINDOW_TOKENS, KEY_VALUE_HEADS, HEAD_SIZE).astype(jnp.float32)
        scores = jnp.einsum('qkgd,skd->kgqs', query_head_rows, key_head_rows) * head_scale
        row_max = jnp.max(jnp.where(visible, scores, -jnp.inf), axis=-1, keepdims=True)
        expd = jnp.where(visible, jnp.exp(scores - row_max), 0.0)
        row_sum = jnp.sum(expd, axis=-1, keepdims=True)
        attn_prob = expd / row_sum
        half_probability = attn_prob.astype(jnp.bfloat16)
        attn_out = jnp.einsum('kgqs,skd->qkgd', half_probability.astype(jnp.float32), value_head_rows).astype(jnp.bfloat16)
        a_flat = attn_out.reshape(WINDOW_TOKENS, QUERY_HEADS * HEAD_SIZE)
        pieces = jnp.einsum('tnc,ncd->tnd', a_flat.reshape(WINDOW_TOKENS, N_SEQ, group_cols).astype(jnp.float32), wo_groups)
        pieces = lax.optimization_barrier(pieces.astype(jnp.bfloat16)).astype(jnp.float32)
        y_out = jnp.sum(pieces, axis=1).astype(jnp.bfloat16)
        wo_grad = wo_grad + jnp.dot(a_flat.T, g_win, preferred_element_type=jnp.float32)
        attention_grad = jnp.dot(g_win, out_weight.T, preferred_element_type=jnp.float32).astype(jnp.bfloat16)
        attention_grad = attention_grad.reshape(WINDOW_TOKENS, KEY_VALUE_HEADS, group_width, HEAD_SIZE).astype(jnp.float32)
        row_dot = jnp.sum(attention_grad * attn_out.astype(jnp.float32), axis=-1)
        row_dot = jnp.transpose(row_dot, (1, 2, 0))[..., None]
        d_prob = jnp.einsum('qkgd,skd->kgqs', attention_grad, value_head_rows)
        score_gradient = (attn_prob * (d_prob - row_dot) * head_scale).astype(jnp.bfloat16).astype(jnp.float32)
        d_q = jnp.einsum('kgqs,skd->qkgd', score_gradient, key_head_rows).astype(jnp.bfloat16).reshape(WINDOW_TOKENS, QUERY_HEADS * HEAD_SIZE)
        key_gradient = jnp.einsum('ubnh,nubr->hur', score_gradient, query_head_rows).astype(jnp.bfloat16).reshape(WINDOW_TOKENS, KEY_VALUE_HEADS * HEAD_SIZE)
        value_gradient = jnp.einsum('ubnh,nubr->hur', half_probability.astype(jnp.float32), attention_grad).astype(jnp.bfloat16).reshape(WINDOW_TOKENS, KEY_VALUE_HEADS * HEAD_SIZE)
        return wo_grad, (y_out, d_q, key_gradient, value_gradient)

    wo_grad, (layer_out, query_grad, key_grad, value_grad) = lax.scan(
        window, jnp.zeros((QUERY_HEADS * HEAD_SIZE, D), jnp.float32),
        (queries, rotated_key_matrix, value_matrix, out_grad, lengths, pack_order))
    return layer_out, query_grad, key_grad, value_grad, wo_grad
```

```python
import jax
import jax.numpy as jnp
from jax import lax
from jax.sharding import Mesh, PartitionSpec as P

QUERY_HEADS = 32
KEY_VALUE_HEADS = 8
HEAD_SIZE = 128
DP = ("dpy", "dpz")


def row_starts(lengths, pack_order, win_rows):
    samples = lengths.shape[0]
    picked = jnp.sum(
        jnp.where(
            pack_order[:, None] == jnp.arange(samples, dtype=jnp.int32)[None, :],
            lengths[None, :],
            0,
        ),
        axis=1,
        dtype=jnp.int32,
    )
    seg_ends = jnp.cumsum(picked, dtype=jnp.int32)
    places = jnp.arange(win_rows, dtype=jnp.int32)
    return jnp.sum(
        jnp.where(seg_ends[None, :] <= places[:, None], picked[None, :], 0), axis=1, dtype=jnp.int32
    )


def local(queries, rotated_key_matrix, value_matrix, out_weight, out_grad, lengths, pack_order):
    row_total_count = queries.shape[1]
    head_scale = HEAD_SIZE ** (-0.5)
    q_tok = queries.reshape(row_total_count, QUERY_HEADS, HEAD_SIZE)
    key_token_rows = rotated_key_matrix.reshape(row_total_count, KEY_VALUE_HEADS, HEAD_SIZE)
    value_token_rows = value_matrix.reshape(row_total_count, KEY_VALUE_HEADS, HEAD_SIZE)
    q_loc, k_loc, v_loc = (
        lax.all_to_all(q_tok, "seq", split_axis=1, concat_axis=0, tiled=True),
        lax.all_to_all(key_token_rows, "seq", split_axis=1, concat_axis=0, tiled=True),
        lax.all_to_all(value_token_rows, "seq", split_axis=1, concat_axis=0, tiled=True),
    )
    win_rows = q_loc.shape[0]
    kv_local = k_loc.shape[1]
    group_width = q_loc.shape[1] // kv_local
    query_head_rows = q_loc.reshape(win_rows, kv_local, group_width, HEAD_SIZE)
    starts = row_starts(lengths[0], pack_order[0], win_rows)
    block_rows = min(512, win_rows)
    blk_count = win_rows // block_rows

    def blk_bounds():
        return (jnp.int32(0), jnp.int32(blk_count))

    def score_tile(q_blk, q_start, k_start):
        k_tile = lax.dynamic_slice_in_dim(k_loc, k_start, block_rows, 0)
        scores = (
            jnp.einsum("qkgd,skd->kgqs", q_blk, k_tile, preferred_element_type=jnp.float32)
            * head_scale
        )
        rows_at = q_start + jnp.arange(block_rows, dtype=jnp.int32)
        cols_at = k_start + jnp.arange(block_rows, dtype=jnp.int32)
        first_at = lax.dynamic_slice_in_dim(starts, q_start, block_rows, 0)
        visible = (cols_at[None, :] >= first_at[:, None]) & (cols_at[None, :] <= rows_at[:, None])
        return (scores, visible)

    def forward_block(blk_index):
        q_start = blk_index * block_rows
        q_blk = lax.dynamic_slice_in_dim(query_head_rows, q_start, block_rows, 0)
        lower_blk, upper_blk = blk_bounds()

        def gather_stats(k_blk, running):
            row_max, row_sum = running
            scores, visible = score_tile(q_blk, q_start, k_blk * block_rows)
            tile_max = jnp.max(jnp.where(visible, scores, -1e30), axis=-1, keepdims=True)
            new_max = jnp.maximum(row_max, tile_max)
            row_sum = row_sum * jnp.exp(row_max - new_max) + jnp.sum(
                jnp.where(visible, jnp.exp(scores - new_max), 0.0), axis=-1, keepdims=True
            )
            return (new_max, row_sum)

        stat_shape = (kv_local, group_width, block_rows, 1)
        row_max, row_sum = lax.fori_loop(
            lower_blk,
            upper_blk,
            gather_stats,
            (jnp.full(stat_shape, -1e30, jnp.float32), jnp.zeros(stat_shape, jnp.float32)),
        )

        def weigh(k_blk, summed):
            k_start = k_blk * block_rows
            scores, visible = score_tile(q_blk, q_start, k_start)
            half_probability = (
                jnp.where(visible, jnp.exp(scores - row_max), 0.0) / row_sum
            ).astype(jnp.bfloat16)
            v_tile = lax.dynamic_slice_in_dim(v_loc, k_start, block_rows, 0)
            return summed + jnp.einsum(
                "kgqs,skd->qkgd", half_probability, v_tile, preferred_element_type=jnp.float32
            )

        summed = lax.fori_loop(
            lower_blk,
            upper_blk,
            weigh,
            jnp.zeros((block_rows, kv_local, group_width, HEAD_SIZE), jnp.float32),
        )
        return (summed.astype(jnp.bfloat16), row_max, row_sum)

    attn_out, max_all, sum_all = lax.map(forward_block, jnp.arange(blk_count, dtype=jnp.int32))
    attn_out = attn_out.reshape(win_rows, kv_local, group_width, HEAD_SIZE)
    a_head = attn_out.reshape(win_rows, kv_local * group_width * HEAD_SIZE)
    grad_rows = out_grad.reshape(row_total_count, out_grad.shape[2])
    a_rows = a_head
    product = jnp.dot(a_rows, out_weight, preferred_element_type=jnp.float32)
    seq_count = lax.psum(1, "seq")
    pieces = product.astype(jnp.bfloat16).reshape(seq_count, win_rows // seq_count, product.shape[1])
    pieces = lax.all_to_all(pieces, "seq", split_axis=0, concat_axis=0, tiled=True)
    y_out = jnp.sum(pieces.astype(jnp.float32), axis=0).astype(jnp.bfloat16)
    incoming = lax.all_gather(grad_rows, "seq", axis=0, tiled=True)
    a_rows = a_head
    wo_grad = lax.dot_general(
        a_rows, incoming, (((0,), (0,)), ((), ())), preferred_element_type=jnp.float32
    )
    d_rows = lax.dot_general(
        incoming, out_weight, (((1,), (1,)), ((), ())), preferred_element_type=jnp.float32
    )
    d_all, wo_grad = (d_rows, wo_grad)
    attention_grad = d_all.astype(jnp.bfloat16).reshape(win_rows, kv_local, group_width, HEAD_SIZE)

    def back_block(blk_index, running):
        dq_all, dk_acc, dv_acc = running
        q_start = blk_index * block_rows
        q_blk = lax.dynamic_slice_in_dim(query_head_rows, q_start, block_rows, 0)
        g_blk = lax.dynamic_slice_in_dim(attention_grad, q_start, block_rows, 0)
        o_blk = lax.dynamic_slice_in_dim(attn_out, q_start, block_rows, 0)
        row_max = max_all[blk_index]
        row_sum = sum_all[blk_index]
        row_dot = jnp.sum(g_blk.astype(jnp.float32) * o_blk.astype(jnp.float32), axis=-1)
        row_dot = jnp.transpose(row_dot, (1, 2, 0))[..., None]
        lower_blk, upper_blk = blk_bounds()

        def per_tile(k_blk, inner):
            dq_acc, dk_run, dv_run = inner
            k_start = k_blk * block_rows
            scores, visible = score_tile(q_blk, q_start, k_start)
            attn_prob = jnp.where(visible, jnp.exp(scores - row_max), 0.0) / row_sum
            k_tile = lax.dynamic_slice_in_dim(k_loc, k_start, block_rows, 0)
            v_tile = lax.dynamic_slice_in_dim(v_loc, k_start, block_rows, 0)
            d_prob = jnp.einsum("qkgd,skd->kgqs", g_blk, v_tile, preferred_element_type=jnp.float32)
            score_gradient = (attn_prob * (d_prob - row_dot) * head_scale).astype(jnp.bfloat16)
            dq_acc = dq_acc + jnp.einsum(
                "kgqs,skd->qkgd", score_gradient, k_tile, preferred_element_type=jnp.float32
            )
            dk_part = jnp.einsum(
                "ubnh,nubr->hur", score_gradient, q_blk, preferred_element_type=jnp.float32
            )
            dv_part = jnp.einsum(
                "ubnh,nubr->hur",
                attn_prob.astype(jnp.bfloat16),
                g_blk,
                preferred_element_type=jnp.float32,
            )
            dk_run = lax.dynamic_update_slice_in_dim(
                dk_run,
                lax.dynamic_slice_in_dim(dk_run, k_start, block_rows, 0) + dk_part,
                k_start,
                0,
            )
            dv_run = lax.dynamic_update_slice_in_dim(
                dv_run,
                lax.dynamic_slice_in_dim(dv_run, k_start, block_rows, 0) + dv_part,
                k_start,
                0,
            )
            return (dq_acc, dk_run, dv_run)

        dq_blk, dk_acc, dv_acc = lax.fori_loop(
            lower_blk,
            upper_blk,
            per_tile,
            (
                jnp.zeros((block_rows, kv_local, group_width, HEAD_SIZE), jnp.float32),
                dk_acc,
                dv_acc,
            ),
        )
        dq_all = lax.dynamic_update_slice_in_dim(dq_all, dq_blk.astype(jnp.bfloat16), q_start, 0)
        return (dq_all, dk_acc, dv_acc)

    dq_all, dk_acc, dv_acc = lax.fori_loop(
        0,
        blk_count,
        back_block,
        (
            jnp.zeros((win_rows, kv_local, group_width, HEAD_SIZE), jnp.bfloat16),
            jnp.zeros((win_rows, kv_local, HEAD_SIZE), jnp.float32),
            jnp.zeros((win_rows, kv_local, HEAD_SIZE), jnp.float32),
        ),
    )
    d_q = dq_all.reshape(win_rows, kv_local * group_width, HEAD_SIZE)
    d_q, key_gradient, value_gradient = (
        lax.all_to_all(d_q, "seq", split_axis=0, concat_axis=1, tiled=True),
        lax.all_to_all(dk_acc.astype(jnp.bfloat16), "seq", split_axis=0, concat_axis=1, tiled=True),
        lax.all_to_all(dv_acc.astype(jnp.bfloat16), "seq", split_axis=0, concat_axis=1, tiled=True),
    )
    y_count = lax.psum(1, "dpy")
    z_count = lax.psum(1, "dpz")
    cols = wo_grad.shape[1]
    wo_perm = (
        wo_grad.reshape(wo_grad.shape[0], y_count, z_count, cols // (y_count * z_count))
        .transpose(0, 2, 1, 3)
        .reshape(wo_grad.shape[0], cols)
    )
    wo_perm = lax.psum_scatter(wo_perm, "dpz", scatter_dimension=1, tiled=True)
    weight_grad = lax.psum_scatter(wo_perm, "dpy", scatter_dimension=1, tiled=True)
    return (
        y_out.reshape(1, row_total_count, y_out.shape[1]),
        d_q.reshape(1, row_total_count, QUERY_HEADS * HEAD_SIZE),
        key_gradient.reshape(1, row_total_count, KEY_VALUE_HEADS * HEAD_SIZE),
        value_gradient.reshape(1, row_total_count, KEY_VALUE_HEADS * HEAD_SIZE),
        weight_grad,
    )


def solution(mesh):
    dp_count = mesh.shape["dp"]
    y_count = 4 if dp_count % 4 == 0 else 1
    mesh = Mesh(
        mesh.devices.reshape(mesh.shape["seq"], y_count, dp_count // y_count), ("seq", "dpy", "dpz")
    )
    in_specs = (
        P(DP, "seq", None),
        P(DP, "seq", None),
        P(DP, "seq", None),
        P("seq", None),
        P(DP, "seq", None),
        P(DP, None),
        P(DP, None),
    )
    out_specs = (
        P(DP, "seq", None),
        P(DP, "seq", None),
        P(DP, "seq", None),
        P(DP, "seq", None),
        P("seq", DP),
    )
    return jax.shard_map(local, mesh=mesh, in_specs=in_specs, out_specs=out_specs, check_vma=False)
```

```python
import jax
import jax.numpy as jnp
from jax import lax
from jax.sharding import Mesh, PartitionSpec as P

QUERY_HEADS = 32
KEY_VALUE_HEADS = 8
HEAD_SIZE = 128
DP = ("dpy", "dpz")
BLOCK = 256
MOST = 256


def row_starts(lengths, pack_order, win_rows):
    samples = lengths.shape[0]
    picked = jnp.sum(
        jnp.where(
            pack_order[:, None] == jnp.arange(samples, dtype=jnp.int32)[None, :],
            lengths[None, :],
            0,
        ),
        axis=1,
        dtype=jnp.int32,
    )
    seg_ends = jnp.cumsum(picked, dtype=jnp.int32)
    places = jnp.arange(win_rows, dtype=jnp.int32)
    return jnp.sum(
        jnp.where(seg_ends[None, :] <= places[:, None], picked[None, :], 0), axis=1, dtype=jnp.int32
    )


def local(queries, rotated_key_matrix, value_matrix, out_weight, out_grad, lengths, pack_order):
    seq_count = lax.psum(1, "seq")
    tok = queries.shape[1]
    head_scale = HEAD_SIZE ** (-0.5)
    hq = QUERY_HEADS // seq_count
    hk = KEY_VALUE_HEADS // seq_count
    group_width = hq // hk
    packed = jnp.concatenate(
        [
            queries.reshape(tok, seq_count, hq, HEAD_SIZE),
            rotated_key_matrix.reshape(tok, seq_count, hk, HEAD_SIZE),
            value_matrix.reshape(tok, seq_count, hk, HEAD_SIZE),
        ],
        axis=2,
    ).transpose(1, 0, 2, 3)
    got = lax.all_to_all(packed, "seq", split_axis=0, concat_axis=0, tiled=True)
    win_rows = seq_count * tok
    got = got.reshape(win_rows, hq + 2 * hk, HEAD_SIZE)
    query_head_rows = got[:, :hq].reshape(win_rows, hk, group_width, HEAD_SIZE)
    k_loc = got[:, hq : hq + hk]
    v_loc = got[:, hq + hk :]
    starts = row_starts(lengths[0], pack_order[0], win_rows)
    blk = min(BLOCK, win_rows)
    blk_count = win_rows // blk
    reach = -(-(MOST - 1) // blk)

    def band(i):
        q_start = i * blk
        k_start = max(0, q_start - reach * blk)
        return q_start, k_start, q_start + blk

    def probs(i, q_blk, m=None, l=None):
        q_start, k_start, k_end = band(i)
        k_band = k_loc[k_start:k_end]
        scores = (
            jnp.einsum("qkgd,skd->kgqs", q_blk, k_band, preferred_element_type=jnp.float32)
            * head_scale
        )
        rows_at = q_start + jnp.arange(blk, dtype=jnp.int32)
        cols_at = k_start + jnp.arange(k_end - k_start, dtype=jnp.int32)
        first_at = starts[q_start : q_start + blk]
        visible = (cols_at[None, :] >= first_at[:, None]) & (cols_at[None, :] <= rows_at[:, None])
        if m is None:
            m = jnp.max(jnp.where(visible, scores, -1e30), axis=-1, keepdims=True)
        expd = jnp.where(visible, jnp.exp(scores - m), 0.0)
        if l is None:
            l = jnp.sum(expd, axis=-1, keepdims=True)
        return expd / l, m, l

    out_blocks, stats = [], []
    for i in range(blk_count):
        q_start, k_start, k_end = band(i)
        q_blk = query_head_rows[q_start : q_start + blk]
        attn_prob, m, l = probs(i, q_blk)
        stats.append((m, l))
        out_blocks.append(
            jnp.einsum(
                "kgqs,skd->qkgd",
                attn_prob.astype(jnp.bfloat16),
                v_loc[k_start:k_end],
                preferred_element_type=jnp.float32,
            ).astype(jnp.bfloat16)
        )
    attn_out = jnp.concatenate(out_blocks, axis=0)
    a_head = attn_out.reshape(win_rows, hq * HEAD_SIZE)
    product = jnp.dot(a_head, out_weight, preferred_element_type=jnp.float32)
    pieces = product.astype(jnp.bfloat16).reshape(seq_count, tok, product.shape[1])
    pieces = lax.all_to_all(pieces, "seq", split_axis=0, concat_axis=0, tiled=True)
    y_out = jnp.sum(pieces.astype(jnp.float32), axis=0).astype(jnp.bfloat16)
    incoming = lax.all_gather(out_grad.reshape(tok, out_grad.shape[2]), "seq", axis=0, tiled=True)
    wo_grad = lax.dot_general(
        a_head, incoming, (((0,), (0,)), ((), ())), preferred_element_type=jnp.float32
    )
    d_rows = lax.dot_general(
        incoming, out_weight, (((1,), (1,)), ((), ())), preferred_element_type=jnp.float32
    )
    attention_grad = d_rows.astype(jnp.bfloat16).reshape(win_rows, hk, group_width, HEAD_SIZE)

    dq_blocks = []
    dk_blocks = [None] * blk_count
    dv_blocks = [None] * blk_count
    for i in range(blk_count):
        q_start, k_start, k_end = band(i)
        q_blk = query_head_rows[q_start : q_start + blk]
        g_blk = attention_grad[q_start : q_start + blk]
        o_blk = attn_out[q_start : q_start + blk]
        row_dot = jnp.sum(g_blk.astype(jnp.float32) * o_blk.astype(jnp.float32), axis=-1)
        row_dot = jnp.transpose(row_dot, (1, 2, 0))[..., None]
        attn_prob, _, _ = probs(i, q_blk, *stats[i])
        k_band = k_loc[k_start:k_end]
        v_band = v_loc[k_start:k_end]
        d_prob = jnp.einsum("qkgd,skd->kgqs", g_blk, v_band, preferred_element_type=jnp.float32)
        score_gradient = (attn_prob * (d_prob - row_dot) * head_scale).astype(jnp.bfloat16)
        dq_blocks.append(
            jnp.einsum(
                "kgqs,skd->qkgd", score_gradient, k_band, preferred_element_type=jnp.float32
            ).astype(jnp.bfloat16)
        )
        dk_part = jnp.einsum(
            "kgqs,qkgd->skd", score_gradient, q_blk, preferred_element_type=jnp.float32
        )
        dv_part = jnp.einsum(
            "kgqs,qkgd->skd",
            attn_prob.astype(jnp.bfloat16),
            g_blk,
            preferred_element_type=jnp.float32,
        )
        for j in range(k_start // blk, k_end // blk):
            lo = j * blk - k_start
            for acc, part in ((dk_blocks, dk_part), (dv_blocks, dv_part)):
                piece = part[lo : lo + blk]
                acc[j] = piece if acc[j] is None else acc[j] + piece
    dq_all = jnp.concatenate(dq_blocks, axis=0).reshape(win_rows, hq, HEAD_SIZE)
    dk_all = jnp.concatenate(dk_blocks, axis=0).astype(jnp.bfloat16)
    dv_all = jnp.concatenate(dv_blocks, axis=0).astype(jnp.bfloat16)
    packed_out = jnp.concatenate([dq_all, dk_all, dv_all], axis=1).reshape(
        seq_count, tok, hq + 2 * hk, HEAD_SIZE
    )
    back = lax.all_to_all(packed_out, "seq", split_axis=0, concat_axis=0, tiled=True)
    back = back.transpose(1, 0, 2, 3)
    d_q = back[:, :, :hq].reshape(1, tok, QUERY_HEADS * HEAD_SIZE)
    key_gradient = back[:, :, hq : hq + hk].reshape(1, tok, KEY_VALUE_HEADS * HEAD_SIZE)
    value_gradient = back[:, :, hq + hk :].reshape(1, tok, KEY_VALUE_HEADS * HEAD_SIZE)
    y_count = lax.psum(1, "dpy")
    z_count = lax.psum(1, "dpz")
    cols = wo_grad.shape[1]
    wo_perm = (
        wo_grad.reshape(wo_grad.shape[0], y_count, z_count, cols // (y_count * z_count))
        .transpose(0, 2, 1, 3)
        .reshape(wo_grad.shape[0], cols)
    )
    wo_perm = lax.psum_scatter(wo_perm, "dpz", scatter_dimension=1, tiled=True)
    weight_grad = lax.psum_scatter(wo_perm, "dpy", scatter_dimension=1, tiled=True)
    return (
        y_out.reshape(1, tok, y_out.shape[1]),
        d_q,
        key_gradient,
        value_gradient,
        weight_grad,
    )


def solution(mesh):
    dp_count = mesh.shape["dp"]
    y_count = 4 if dp_count % 4 == 0 else 1
    mesh = Mesh(
        mesh.devices.reshape(mesh.shape["seq"], y_count, dp_count // y_count), ("seq", "dpy", "dpz")
    )
    in_specs = (
        P(DP, "seq", None),
        P(DP, "seq", None),
        P(DP, "seq", None),
        P("seq", None),
        P(DP, "seq", None),
        P(DP, None),
        P(DP, None),
    )
    out_specs = (
        P(DP, "seq", None),
        P(DP, "seq", None),
        P(DP, "seq", None),
        P(DP, "seq", None),
        P("seq", DP),
    )
    return jax.shard_map(local, mesh=mesh, in_specs=in_specs, out_specs=out_specs, check_vma=False)
```

```python
import jax
import jax.numpy as jnp
from jax import lax
from jax.sharding import Mesh, PartitionSpec as P

QUERY_HEADS = 32
KEY_VALUE_HEADS = 8
HEAD_SIZE = 128
DP = ("dpy", "dpz")
SEQ = ("x", "core")
BLOCK = 256
MOST = 256


def row_starts(lengths, pack_order, win_rows):
    samples = lengths.shape[0]
    picked = jnp.sum(
        jnp.where(
            pack_order[:, None] == jnp.arange(samples, dtype=jnp.int32)[None, :],
            lengths[None, :],
            0,
        ),
        axis=1,
        dtype=jnp.int32,
    )
    seg_ends = jnp.cumsum(picked, dtype=jnp.int32)
    places = jnp.arange(win_rows, dtype=jnp.int32)
    return jnp.sum(
        jnp.where(seg_ends[None, :] <= places[:, None], picked[None, :], 0), axis=1, dtype=jnp.int32
    )


def local(queries, rotated_key_matrix, value_matrix, out_weight, out_grad, lengths, pack_order):
    seq_count = lax.psum(1, SEQ)
    x_count = lax.psum(1, "x")
    core_count = lax.psum(1, "core")
    tok = queries.shape[1]
    head_scale = HEAD_SIZE ** (-0.5)
    hq = QUERY_HEADS // seq_count
    hk = KEY_VALUE_HEADS // seq_count
    group_width = hq // hk
    packed = jnp.concatenate(
        [
            queries.reshape(tok, seq_count, hq, HEAD_SIZE),
            rotated_key_matrix.reshape(tok, seq_count, hk, HEAD_SIZE),
            value_matrix.reshape(tok, seq_count, hk, HEAD_SIZE),
        ],
        axis=2,
    ).transpose(1, 0, 2, 3)
    got = lax.all_to_all(packed, SEQ, split_axis=0, concat_axis=0, tiled=True)
    got, out_grad = lax.optimization_barrier((got, out_grad))
    win_rows = seq_count * tok
    got = got.reshape(win_rows, hq + 2 * hk, HEAD_SIZE)
    query_head_rows = got[:, :hq].reshape(win_rows, hk, group_width, HEAD_SIZE)
    k_loc = got[:, hq : hq + hk]
    v_loc = got[:, hq + hk :]
    starts = row_starts(lengths[0], pack_order[0], win_rows)
    blk = min(BLOCK, win_rows)
    blk_count = win_rows // blk
    reach = -(-(MOST - 1) // blk)

    def band(i):
        q_start = i * blk
        k_start = max(0, q_start - reach * blk)
        return q_start, k_start, q_start + blk

    def probs(i, q_blk, m=None, l=None):
        q_start, k_start, k_end = band(i)
        k_band = k_loc[k_start:k_end]
        scores = (
            jnp.einsum("qkgd,skd->kgqs", q_blk, k_band, preferred_element_type=jnp.float32)
            * head_scale
        )
        rows_at = q_start + jnp.arange(blk, dtype=jnp.int32)
        cols_at = k_start + jnp.arange(k_end - k_start, dtype=jnp.int32)
        first_at = starts[q_start : q_start + blk]
        visible = (cols_at[None, :] >= first_at[:, None]) & (cols_at[None, :] <= rows_at[:, None])
        if m is None:
            m = jnp.max(jnp.where(visible, scores, -1e30), axis=-1, keepdims=True)
        expd = jnp.where(visible, jnp.exp(scores - m), 0.0)
        if l is None:
            l = jnp.sum(expd, axis=-1, keepdims=True)
        return expd / l, m, l

    out_blocks, stats = [], []
    for i in range(blk_count):
        q_start, k_start, k_end = band(i)
        q_blk = query_head_rows[q_start : q_start + blk]
        attn_prob, m, l = probs(i, q_blk)
        stats.append((m, l))
        out_blocks.append(
            jnp.einsum(
                "kgqs,skd->qkgd",
                attn_prob.astype(jnp.bfloat16),
                v_loc[k_start:k_end],
                preferred_element_type=jnp.float32,
            ).astype(jnp.bfloat16)
        )
    attn_out = jnp.concatenate(out_blocks, axis=0)
    a_head = attn_out.reshape(win_rows, hq * HEAD_SIZE)
    product = jnp.dot(a_head, out_weight, preferred_element_type=jnp.float32)
    width = product.shape[1]
    pieces = (
        product.astype(jnp.bfloat16)
        .reshape(x_count, core_count, tok, width)
        .transpose(1, 0, 2, 3)
    )
    pieces = lax.all_to_all(pieces, "core", split_axis=0, concat_axis=0, tiled=True)
    pair_sum = jnp.sum(pieces.astype(jnp.float32), axis=0).astype(jnp.bfloat16)
    pair_sum = lax.all_to_all(pair_sum, "x", split_axis=0, concat_axis=0, tiled=True)
    y_out = jnp.sum(pair_sum.astype(jnp.float32), axis=0).astype(jnp.bfloat16)
    g_rows = lax.all_gather(out_grad.reshape(tok, out_grad.shape[2]), "x", axis=0, tiled=False)
    g_rows = lax.all_gather(g_rows, "core", axis=0, tiled=False)
    incoming = g_rows.transpose(1, 0, 2, 3).reshape(win_rows, g_rows.shape[3])
    wo_grad = lax.dot_general(
        a_head, incoming, (((0,), (0,)), ((), ())), preferred_element_type=jnp.float32
    )
    d_rows = lax.dot_general(
        incoming, out_weight, (((1,), (1,)), ((), ())), preferred_element_type=jnp.float32
    )
    attention_grad = d_rows.astype(jnp.bfloat16).reshape(win_rows, hk, group_width, HEAD_SIZE)

    dq_blocks = []
    dk_blocks = [None] * blk_count
    dv_blocks = [None] * blk_count
    for i in range(blk_count):
        q_start, k_start, k_end = band(i)
        q_blk = query_head_rows[q_start : q_start + blk]
        g_blk = attention_grad[q_start : q_start + blk]
        o_blk = attn_out[q_start : q_start + blk]
        row_dot = jnp.sum(g_blk.astype(jnp.float32) * o_blk.astype(jnp.float32), axis=-1)
        row_dot = jnp.transpose(row_dot, (1, 2, 0))[..., None]
        attn_prob, _, _ = probs(i, q_blk, *stats[i])
        k_band = k_loc[k_start:k_end]
        v_band = v_loc[k_start:k_end]
        d_prob = jnp.einsum("qkgd,skd->kgqs", g_blk, v_band, preferred_element_type=jnp.float32)
        score_gradient = (attn_prob * (d_prob - row_dot) * head_scale).astype(jnp.bfloat16)
        dq_blocks.append(
            jnp.einsum(
                "kgqs,skd->qkgd", score_gradient, k_band, preferred_element_type=jnp.float32
            ).astype(jnp.bfloat16)
        )
        dk_part = jnp.einsum(
            "kgqs,qkgd->skd", score_gradient, q_blk, preferred_element_type=jnp.float32
        )
        dv_part = jnp.einsum(
            "kgqs,qkgd->skd",
            attn_prob.astype(jnp.bfloat16),
            g_blk,
            preferred_element_type=jnp.float32,
        )
        for j in range(k_start // blk, k_end // blk):
            lo = j * blk - k_start
            for acc, part in ((dk_blocks, dk_part), (dv_blocks, dv_part)):
                piece = part[lo : lo + blk]
                acc[j] = piece if acc[j] is None else acc[j] + piece
    dq_all = jnp.concatenate(dq_blocks, axis=0).reshape(win_rows, hq, HEAD_SIZE)
    dk_all = jnp.concatenate(dk_blocks, axis=0).astype(jnp.bfloat16)
    dv_all = jnp.concatenate(dv_blocks, axis=0).astype(jnp.bfloat16)
    packed_out = jnp.concatenate([dq_all, dk_all, dv_all], axis=1).reshape(
        seq_count, tok, hq + 2 * hk, HEAD_SIZE
    )
    back = lax.all_to_all(packed_out, SEQ, split_axis=0, concat_axis=0, tiled=True)
    back = back.transpose(1, 0, 2, 3)
    d_q = back[:, :, :hq].reshape(1, tok, QUERY_HEADS * HEAD_SIZE)
    key_gradient = back[:, :, hq : hq + hk].reshape(1, tok, KEY_VALUE_HEADS * HEAD_SIZE)
    value_gradient = back[:, :, hq + hk :].reshape(1, tok, KEY_VALUE_HEADS * HEAD_SIZE)
    y_count = lax.psum(1, "dpy")
    z_count = lax.psum(1, "dpz")
    cols = wo_grad.shape[1]
    wo_perm = (
        wo_grad.reshape(wo_grad.shape[0], y_count, z_count, cols // (y_count * z_count))
        .transpose(0, 2, 1, 3)
        .reshape(wo_grad.shape[0], cols)
    )
    wo_perm = lax.psum_scatter(wo_perm, "dpz", scatter_dimension=1, tiled=True)
    weight_grad = lax.psum_scatter(wo_perm, "dpy", scatter_dimension=1, tiled=True)
    return (
        y_out.reshape(1, tok, y_out.shape[1]),
        d_q,
        key_gradient,
        value_gradient,
        weight_grad,
    )


def solution(mesh):
    dp_count = mesh.shape["dp"]
    y_count = 4 if dp_count % 4 == 0 else 1
    seq_count = mesh.shape["seq"]
    core_count = 2 if seq_count % 2 == 0 else 1
    mesh = Mesh(
        mesh.devices.reshape(
            seq_count // core_count, core_count, y_count, dp_count // y_count
        ),
        ("x", "core", "dpy", "dpz"),
    )
    in_specs = (
        P(DP, SEQ, None),
        P(DP, SEQ, None),
        P(DP, SEQ, None),
        P(SEQ, None),
        P(DP, SEQ, None),
        P(DP, None),
        P(DP, None),
    )
    out_specs = (
        P(DP, SEQ, None),
        P(DP, SEQ, None),
        P(DP, SEQ, None),
        P(DP, SEQ, None),
        P(SEQ, DP),
    )
    return jax.shard_map(local, mesh=mesh, in_specs=in_specs, out_specs=out_specs, check_vma=False)
```

```python
import jax
import jax.numpy as jnp
from jax import lax
from jax.sharding import Mesh, PartitionSpec as P

QUERY_HEADS = 32
KEY_VALUE_HEADS = 8
HEAD_SIZE = 128
DP = ("dpy", "dpz")
BLOCK = 256
MOST = 256


def row_starts(lengths, pack_order, win_rows):
    samples = lengths.shape[0]
    picked = jnp.sum(
        jnp.where(
            pack_order[:, None] == jnp.arange(samples, dtype=jnp.int32)[None, :],
            lengths[None, :],
            0,
        ),
        axis=1,
        dtype=jnp.int32,
    )
    seg_ends = jnp.cumsum(picked, dtype=jnp.int32)
    places = jnp.arange(win_rows, dtype=jnp.int32)
    return jnp.sum(
        jnp.where(seg_ends[None, :] <= places[:, None], picked[None, :], 0), axis=1, dtype=jnp.int32
    )


def local(queries, rotated_key_matrix, value_matrix, out_weight, out_grad, lengths, pack_order):
    seq_count = lax.psum(1, "seq")
    tok = queries.shape[1]
    head_scale = HEAD_SIZE ** (-0.5)
    hq = QUERY_HEADS // seq_count
    hk = KEY_VALUE_HEADS // seq_count
    group_width = hq // hk
    win_rows = seq_count * tok
    query_head_rows, k_loc, v_loc = (
        lax.all_to_all(
            queries.reshape(tok, QUERY_HEADS, HEAD_SIZE), "seq", split_axis=1, concat_axis=0, tiled=True
        ).reshape(win_rows, hk, group_width, HEAD_SIZE),
        lax.all_to_all(
            rotated_key_matrix.reshape(tok, KEY_VALUE_HEADS, HEAD_SIZE),
            "seq",
            split_axis=1,
            concat_axis=0,
            tiled=True,
        ),
        lax.all_to_all(
            value_matrix.reshape(tok, KEY_VALUE_HEADS, HEAD_SIZE),
            "seq",
            split_axis=1,
            concat_axis=0,
            tiled=True,
        ),
    )
    starts = row_starts(lengths[0], pack_order[0], win_rows)
    blk = min(BLOCK, win_rows)
    blk_count = win_rows // blk
    reach = -(-(MOST - 1) // blk)

    def band(i):
        q_start = i * blk
        k_start = max(0, q_start - reach * blk)
        return q_start, k_start, q_start + blk

    def probs(i, q_blk, m=None, l=None):
        q_start, k_start, k_end = band(i)
        k_band = k_loc[k_start:k_end]
        scores = (
            jnp.einsum("qkgd,skd->kgqs", q_blk, k_band, preferred_element_type=jnp.float32)
            * head_scale
        )
        rows_at = q_start + jnp.arange(blk, dtype=jnp.int32)
        cols_at = k_start + jnp.arange(k_end - k_start, dtype=jnp.int32)
        first_at = starts[q_start : q_start + blk]
        visible = (cols_at[None, :] >= first_at[:, None]) & (cols_at[None, :] <= rows_at[:, None])
        if m is None:
            m = jnp.max(jnp.where(visible, scores, -1e30), axis=-1, keepdims=True)
        expd = jnp.where(visible, jnp.exp(scores - m), 0.0)
        if l is None:
            l = jnp.sum(expd, axis=-1, keepdims=True)
        return expd / l, m, l

    out_blocks, stats = [], []
    for i in range(blk_count):
        q_start, k_start, k_end = band(i)
        q_blk = query_head_rows[q_start : q_start + blk]
        attn_prob, m, l = probs(i, q_blk)
        stats.append((m, l))
        out_blocks.append(
            jnp.einsum(
                "kgqs,skd->qkgd",
                attn_prob.astype(jnp.bfloat16),
                v_loc[k_start:k_end],
                preferred_element_type=jnp.float32,
            ).astype(jnp.bfloat16)
        )
    attn_out = jnp.concatenate(out_blocks, axis=0)
    a_head = attn_out.reshape(win_rows, hq * HEAD_SIZE)
    product = jnp.dot(a_head, out_weight, preferred_element_type=jnp.float32)
    pieces = product.astype(jnp.bfloat16).reshape(seq_count, tok, product.shape[1])
    pieces = lax.all_to_all(pieces, "seq", split_axis=0, concat_axis=0, tiled=True)
    y_out = jnp.sum(pieces.astype(jnp.float32), axis=0).astype(jnp.bfloat16)
    incoming = lax.all_gather(out_grad.reshape(tok, out_grad.shape[2]), "seq", axis=0, tiled=True)
    wo_grad = lax.dot_general(
        a_head, incoming, (((0,), (0,)), ((), ())), preferred_element_type=jnp.float32
    )
    d_rows = lax.dot_general(
        incoming, out_weight, (((1,), (1,)), ((), ())), preferred_element_type=jnp.float32
    )
    attention_grad = d_rows.astype(jnp.bfloat16).reshape(win_rows, hk, group_width, HEAD_SIZE)

    dq_blocks = []
    dk_blocks = [None] * blk_count
    dv_blocks = [None] * blk_count
    for i in range(blk_count):
        q_start, k_start, k_end = band(i)
        q_blk = query_head_rows[q_start : q_start + blk]
        g_blk = attention_grad[q_start : q_start + blk]
        o_blk = attn_out[q_start : q_start + blk]
        row_dot = jnp.sum(g_blk.astype(jnp.float32) * o_blk.astype(jnp.float32), axis=-1)
        row_dot = jnp.transpose(row_dot, (1, 2, 0))[..., None]
        attn_prob, _, _ = probs(i, q_blk, *stats[i])
        k_band = k_loc[k_start:k_end]
        v_band = v_loc[k_start:k_end]
        d_prob = jnp.einsum("qkgd,skd->kgqs", g_blk, v_band, preferred_element_type=jnp.float32)
        score_gradient = (attn_prob * (d_prob - row_dot) * head_scale).astype(jnp.bfloat16)
        dq_blocks.append(
            jnp.einsum(
                "kgqs,skd->qkgd", score_gradient, k_band, preferred_element_type=jnp.float32
            ).astype(jnp.bfloat16)
        )
        dk_part = jnp.einsum(
            "kgqs,qkgd->skd", score_gradient, q_blk, preferred_element_type=jnp.float32
        )
        dv_part = jnp.einsum(
            "kgqs,qkgd->skd",
            attn_prob.astype(jnp.bfloat16),
            g_blk,
            preferred_element_type=jnp.float32,
        )
        for j in range(k_start // blk, k_end // blk):
            lo = j * blk - k_start
            for acc, part in ((dk_blocks, dk_part), (dv_blocks, dv_part)):
                piece = part[lo : lo + blk]
                acc[j] = piece if acc[j] is None else acc[j] + piece
    dq_all = jnp.concatenate(dq_blocks, axis=0).reshape(win_rows, hq, HEAD_SIZE)
    dk_all = jnp.concatenate(dk_blocks, axis=0).astype(jnp.bfloat16)
    dv_all = jnp.concatenate(dv_blocks, axis=0).astype(jnp.bfloat16)
    d_q, key_gradient, value_gradient = (
        lax.all_to_all(dq_all, "seq", split_axis=0, concat_axis=1, tiled=True),
        lax.all_to_all(dk_all, "seq", split_axis=0, concat_axis=1, tiled=True),
        lax.all_to_all(dv_all, "seq", split_axis=0, concat_axis=1, tiled=True),
    )
    d_q = d_q.reshape(1, tok, QUERY_HEADS * HEAD_SIZE)
    key_gradient = key_gradient.reshape(1, tok, KEY_VALUE_HEADS * HEAD_SIZE)
    value_gradient = value_gradient.reshape(1, tok, KEY_VALUE_HEADS * HEAD_SIZE)
    y_count = lax.psum(1, "dpy")
    z_count = lax.psum(1, "dpz")
    cols = wo_grad.shape[1]
    wo_perm = (
        wo_grad.reshape(wo_grad.shape[0], y_count, z_count, cols // (y_count * z_count))
        .transpose(0, 2, 1, 3)
        .reshape(wo_grad.shape[0], cols)
    )
    wo_perm = lax.psum_scatter(wo_perm, "dpz", scatter_dimension=1, tiled=True)
    weight_grad = lax.psum_scatter(wo_perm, "dpy", scatter_dimension=1, tiled=True)
    return (
        y_out.reshape(1, tok, y_out.shape[1]),
        d_q,
        key_gradient,
        value_gradient,
        weight_grad,
    )


def solution(mesh):
    dp_count = mesh.shape["dp"]
    y_count = 4 if dp_count % 4 == 0 else 1
    mesh = Mesh(
        mesh.devices.reshape(mesh.shape["seq"], y_count, dp_count // y_count), ("seq", "dpy", "dpz")
    )
    in_specs = (
        P(DP, "seq", None),
        P(DP, "seq", None),
        P(DP, "seq", None),
        P("seq", None),
        P(DP, "seq", None),
        P(DP, None),
        P(DP, None),
    )
    out_specs = (
        P(DP, "seq", None),
        P(DP, "seq", None),
        P(DP, "seq", None),
        P(DP, "seq", None),
        P("seq", DP),
    )
    return jax.shard_map(local, mesh=mesh, in_specs=in_specs, out_specs=out_specs, check_vma=False)
```

```python
import jax
import jax.numpy as jnp
from jax import lax
from jax.sharding import Mesh, PartitionSpec as P

QUERY_HEADS = 32
KEY_VALUE_HEADS = 8
HEAD_SIZE = 128
DP = ("dpy", "dpz")
BLOCK = 256
MOST = 256


def row_starts(lengths, pack_order, win_rows):
    samples = lengths.shape[0]
    picked = jnp.sum(
        jnp.where(
            pack_order[:, None] == jnp.arange(samples, dtype=jnp.int32)[None, :],
            lengths[None, :],
            0,
        ),
        axis=1,
        dtype=jnp.int32,
    )
    seg_ends = jnp.cumsum(picked, dtype=jnp.int32)
    places = jnp.arange(win_rows, dtype=jnp.int32)
    return jnp.sum(
        jnp.where(seg_ends[None, :] <= places[:, None], picked[None, :], 0), axis=1, dtype=jnp.int32
    )


def local(queries, rotated_key_matrix, value_matrix, out_weight, out_grad, lengths, pack_order):
    seq_count = lax.psum(1, "seq")
    tok = queries.shape[1]
    head_scale = HEAD_SIZE ** (-0.5)
    hq = QUERY_HEADS // seq_count
    hk = KEY_VALUE_HEADS // seq_count
    group_width = hq // hk
    packed = jnp.concatenate(
        [
            queries.reshape(tok, seq_count, hq, HEAD_SIZE),
            rotated_key_matrix.reshape(tok, seq_count, hk, HEAD_SIZE),
            value_matrix.reshape(tok, seq_count, hk, HEAD_SIZE),
        ],
        axis=2,
    ).transpose(1, 0, 2, 3)
    got = lax.all_to_all(packed, "seq", split_axis=0, concat_axis=0, tiled=True)
    win_rows = seq_count * tok
    got = got.reshape(win_rows, hq + 2 * hk, HEAD_SIZE)
    query_head_rows = got[:, :hq].reshape(win_rows, hk, group_width, HEAD_SIZE)
    k_loc = got[:, hq : hq + hk]
    v_loc = got[:, hq + hk :]
    starts = row_starts(lengths[0], pack_order[0], win_rows)
    blk = min(BLOCK, win_rows)
    blk_count = win_rows // blk
    reach = -(-(MOST - 1) // blk)

    def band(i):
        q_start = i * blk
        k_start = max(0, q_start - reach * blk)
        return q_start, k_start, q_start + blk

    def probs(i, q_blk, m=None, l=None):
        q_start, k_start, k_end = band(i)
        k_band = k_loc[k_start:k_end]
        scores = (
            jnp.einsum("qkgd,skd->kgqs", q_blk, k_band, preferred_element_type=jnp.float32)
            * head_scale
        )
        rows_at = q_start + jnp.arange(blk, dtype=jnp.int32)
        cols_at = k_start + jnp.arange(k_end - k_start, dtype=jnp.int32)
        first_at = starts[q_start : q_start + blk]
        visible = (cols_at[None, :] >= first_at[:, None]) & (cols_at[None, :] <= rows_at[:, None])
        if m is None:
            m = jnp.max(jnp.where(visible, scores, -1e30), axis=-1, keepdims=True)
        expd = jnp.where(visible, jnp.exp(scores - m), 0.0)
        if l is None:
            l = jnp.sum(expd, axis=-1, keepdims=True)
        return expd / l, m, l

    out_blocks, stats = [], []
    for i in range(blk_count):
        q_start, k_start, k_end = band(i)
        q_blk = query_head_rows[q_start : q_start + blk]
        attn_prob, m, l = probs(i, q_blk)
        stats.append((m, l))
        out_blocks.append(
            jnp.einsum(
                "kgqs,skd->qkgd",
                attn_prob.astype(jnp.bfloat16),
                v_loc[k_start:k_end],
                preferred_element_type=jnp.float32,
            ).astype(jnp.bfloat16)
        )
    attn_out = jnp.concatenate(out_blocks, axis=0)
    a_head = attn_out.reshape(win_rows, hq * HEAD_SIZE)
    product = jnp.dot(a_head, out_weight, preferred_element_type=jnp.float32)
    pieces = product.astype(jnp.bfloat16).reshape(seq_count, tok, product.shape[1])
    incoming = lax.all_gather(out_grad.reshape(tok, out_grad.shape[2]), "seq", axis=0, tiled=True)
    wo_grad = lax.dot_general(
        a_head, incoming, (((0,), (0,)), ((), ())), preferred_element_type=jnp.float32
    )
    d_rows = lax.dot_general(
        incoming, out_weight, (((1,), (1,)), ((), ())), preferred_element_type=jnp.float32
    )
    attention_grad = d_rows.astype(jnp.bfloat16).reshape(win_rows, hk, group_width, HEAD_SIZE)
    pieces, attention_grad = lax.optimization_barrier((pieces, attention_grad))
    pieces = lax.all_to_all(pieces, "seq", split_axis=0, concat_axis=0, tiled=True)

    dq_blocks = []
    dk_blocks = [None] * blk_count
    dv_blocks = [None] * blk_count
    for i in range(blk_count):
        if i == blk_count // 2:
            pieces, attention_grad = lax.optimization_barrier((pieces, attention_grad))
        q_start, k_start, k_end = band(i)
        q_blk = query_head_rows[q_start : q_start + blk]
        g_blk = attention_grad[q_start : q_start + blk]
        o_blk = attn_out[q_start : q_start + blk]
        row_dot = jnp.sum(g_blk.astype(jnp.float32) * o_blk.astype(jnp.float32), axis=-1)
        row_dot = jnp.transpose(row_dot, (1, 2, 0))[..., None]
        attn_prob, _, _ = probs(i, q_blk, *stats[i])
        k_band = k_loc[k_start:k_end]
        v_band = v_loc[k_start:k_end]
        d_prob = jnp.einsum("qkgd,skd->kgqs", g_blk, v_band, preferred_element_type=jnp.float32)
        score_gradient = (attn_prob * (d_prob - row_dot) * head_scale).astype(jnp.bfloat16)
        dq_blocks.append(
            jnp.einsum(
                "kgqs,skd->qkgd", score_gradient, k_band, preferred_element_type=jnp.float32
            ).astype(jnp.bfloat16)
        )
        dk_part = jnp.einsum(
            "kgqs,qkgd->skd", score_gradient, q_blk, preferred_element_type=jnp.float32
        )
        dv_part = jnp.einsum(
            "kgqs,qkgd->skd",
            attn_prob.astype(jnp.bfloat16),
            g_blk,
            preferred_element_type=jnp.float32,
        )
        for j in range(k_start // blk, k_end // blk):
            lo = j * blk - k_start
            for acc, part in ((dk_blocks, dk_part), (dv_blocks, dv_part)):
                piece = part[lo : lo + blk]
                acc[j] = piece if acc[j] is None else acc[j] + piece
    y_out = jnp.sum(pieces.astype(jnp.float32), axis=0).astype(jnp.bfloat16)
    dq_all = jnp.concatenate(dq_blocks, axis=0).reshape(win_rows, hq, HEAD_SIZE)
    dk_all = jnp.concatenate(dk_blocks, axis=0).astype(jnp.bfloat16)
    dv_all = jnp.concatenate(dv_blocks, axis=0).astype(jnp.bfloat16)
    packed_out = jnp.concatenate([dq_all, dk_all, dv_all], axis=1).reshape(
        seq_count, tok, hq + 2 * hk, HEAD_SIZE
    )
    back = lax.all_to_all(packed_out, "seq", split_axis=0, concat_axis=0, tiled=True)
    back = back.transpose(1, 0, 2, 3)
    d_q = back[:, :, :hq].reshape(1, tok, QUERY_HEADS * HEAD_SIZE)
    key_gradient = back[:, :, hq : hq + hk].reshape(1, tok, KEY_VALUE_HEADS * HEAD_SIZE)
    value_gradient = back[:, :, hq + hk :].reshape(1, tok, KEY_VALUE_HEADS * HEAD_SIZE)
    y_count = lax.psum(1, "dpy")
    z_count = lax.psum(1, "dpz")
    cols = wo_grad.shape[1]
    wo_perm = (
        wo_grad.reshape(wo_grad.shape[0], y_count, z_count, cols // (y_count * z_count))
        .transpose(0, 2, 1, 3)
        .reshape(wo_grad.shape[0], cols)
    )
    wo_perm = lax.psum_scatter(wo_perm, "dpz", scatter_dimension=1, tiled=True)
    weight_grad = lax.psum_scatter(wo_perm, "dpy", scatter_dimension=1, tiled=True)
    return (
        y_out.reshape(1, tok, y_out.shape[1]),
        d_q,
        key_gradient,
        value_gradient,
        weight_grad,
    )


def solution(mesh):
    dp_count = mesh.shape["dp"]
    y_count = 4 if dp_count % 4 == 0 else 1
    mesh = Mesh(
        mesh.devices.reshape(mesh.shape["seq"], y_count, dp_count // y_count), ("seq", "dpy", "dpz")
    )
    in_specs = (
        P(DP, "seq", None),
        P(DP, "seq", None),
        P(DP, "seq", None),
        P("seq", None),
        P(DP, "seq", None),
        P(DP, None),
        P(DP, None),
    )
    out_specs = (
        P(DP, "seq", None),
        P(DP, "seq", None),
        P(DP, "seq", None),
        P(DP, "seq", None),
        P("seq", DP),
    )
    return jax.shard_map(local, mesh=mesh, in_specs=in_specs, out_specs=out_specs, check_vma=False)
```

```python
import jax
import jax.numpy as jnp
from jax import lax
from jax.sharding import Mesh, PartitionSpec as P

QUERY_HEADS = 32
KEY_VALUE_HEADS = 8
HEAD_SIZE = 128
DP = ("dpy", "dpz")
SEQ = ("x", "core")
BLOCK = 256
MOST = 256


def row_starts(lengths, pack_order, win_rows):
    samples = lengths.shape[0]
    picked = jnp.sum(
        jnp.where(
            pack_order[:, None] == jnp.arange(samples, dtype=jnp.int32)[None, :],
            lengths[None, :],
            0,
        ),
        axis=1,
        dtype=jnp.int32,
    )
    seg_ends = jnp.cumsum(picked, dtype=jnp.int32)
    places = jnp.arange(win_rows, dtype=jnp.int32)
    return jnp.sum(
        jnp.where(seg_ends[None, :] <= places[:, None], picked[None, :], 0), axis=1, dtype=jnp.int32
    )


def local(queries, rotated_key_matrix, value_matrix, out_weight, out_grad, lengths, pack_order):
    seq_count = lax.psum(1, SEQ)
    x_count = lax.psum(1, "x")
    core_count = lax.psum(1, "core")
    tok = queries.shape[1]
    head_scale = HEAD_SIZE ** (-0.5)
    hq = QUERY_HEADS // seq_count
    hk = KEY_VALUE_HEADS // seq_count
    group_width = hq // hk
    packed = jnp.concatenate(
        [
            queries.reshape(tok, seq_count, hq, HEAD_SIZE),
            rotated_key_matrix.reshape(tok, seq_count, hk, HEAD_SIZE),
            value_matrix.reshape(tok, seq_count, hk, HEAD_SIZE),
        ],
        axis=2,
    ).transpose(1, 0, 2, 3)
    got = lax.all_to_all(packed, SEQ, split_axis=0, concat_axis=0, tiled=True)
    win_rows = seq_count * tok
    got = got.reshape(win_rows, hq + 2 * hk, HEAD_SIZE)
    query_head_rows = got[:, :hq].reshape(win_rows, hk, group_width, HEAD_SIZE)
    k_loc = got[:, hq : hq + hk]
    v_loc = got[:, hq + hk :]
    starts = row_starts(lengths[0], pack_order[0], win_rows)
    blk = min(BLOCK, win_rows)
    blk_count = win_rows // blk
    reach = -(-(MOST - 1) // blk)

    def band(i):
        q_start = i * blk
        k_start = max(0, q_start - reach * blk)
        return q_start, k_start, q_start + blk

    def probs(i, q_blk, m=None, l=None):
        q_start, k_start, k_end = band(i)
        k_band = k_loc[k_start:k_end]
        scores = (
            jnp.einsum("qkgd,skd->kgqs", q_blk, k_band, preferred_element_type=jnp.float32)
            * head_scale
        )
        rows_at = q_start + jnp.arange(blk, dtype=jnp.int32)
        cols_at = k_start + jnp.arange(k_end - k_start, dtype=jnp.int32)
        first_at = starts[q_start : q_start + blk]
        visible = (cols_at[None, :] >= first_at[:, None]) & (cols_at[None, :] <= rows_at[:, None])
        if m is None:
            m = jnp.max(jnp.where(visible, scores, -1e30), axis=-1, keepdims=True)
        expd = jnp.where(visible, jnp.exp(scores - m), 0.0)
        if l is None:
            l = jnp.sum(expd, axis=-1, keepdims=True)
        return expd / l, m, l

    out_blocks, stats = [], []
    for i in range(blk_count):
        q_start, k_start, k_end = band(i)
        q_blk = query_head_rows[q_start : q_start + blk]
        attn_prob, m, l = probs(i, q_blk)
        stats.append((m, l))
        out_blocks.append(
            jnp.einsum(
                "kgqs,skd->qkgd",
                attn_prob.astype(jnp.bfloat16),
                v_loc[k_start:k_end],
                preferred_element_type=jnp.float32,
            ).astype(jnp.bfloat16)
        )
    attn_out = jnp.concatenate(out_blocks, axis=0)
    a_head = attn_out.reshape(win_rows, hq * HEAD_SIZE)
    product = jnp.dot(a_head, out_weight, preferred_element_type=jnp.float32)
    pieces = (
        product.astype(jnp.bfloat16)
        .reshape(x_count, core_count, tok, product.shape[1])
        .transpose(1, 0, 2, 3)
    )
    incoming = lax.all_gather(out_grad.reshape(tok, out_grad.shape[2]), SEQ, axis=0, tiled=True)
    wo_grad = lax.dot_general(
        a_head, incoming, (((0,), (0,)), ((), ())), preferred_element_type=jnp.float32
    )
    d_rows = lax.dot_general(
        incoming, out_weight, (((1,), (1,)), ((), ())), preferred_element_type=jnp.float32
    )
    attention_grad = d_rows.astype(jnp.bfloat16).reshape(win_rows, hk, group_width, HEAD_SIZE)
    pieces, attention_grad = lax.optimization_barrier((pieces, attention_grad))
    pieces = lax.all_to_all(pieces, "core", split_axis=0, concat_axis=0, tiled=True)
    pieces = jnp.sum(pieces.astype(jnp.float32), axis=0).astype(jnp.bfloat16)
    pieces = lax.all_to_all(pieces, "x", split_axis=0, concat_axis=0, tiled=True)

    dq_blocks = []
    dk_blocks = [None] * blk_count
    dv_blocks = [None] * blk_count
    for i in range(blk_count):
        if i == blk_count // 2:
            pieces, attention_grad = lax.optimization_barrier((pieces, attention_grad))
        q_start, k_start, k_end = band(i)
        q_blk = query_head_rows[q_start : q_start + blk]
        g_blk = attention_grad[q_start : q_start + blk]
        o_blk = attn_out[q_start : q_start + blk]
        row_dot = jnp.sum(g_blk.astype(jnp.float32) * o_blk.astype(jnp.float32), axis=-1)
        row_dot = jnp.transpose(row_dot, (1, 2, 0))[..., None]
        attn_prob, _, _ = probs(i, q_blk, *stats[i])
        k_band = k_loc[k_start:k_end]
        v_band = v_loc[k_start:k_end]
        d_prob = jnp.einsum("qkgd,skd->kgqs", g_blk, v_band, preferred_element_type=jnp.float32)
        score_gradient = (attn_prob * (d_prob - row_dot) * head_scale).astype(jnp.bfloat16)
        dq_blocks.append(
            jnp.einsum(
                "kgqs,skd->qkgd", score_gradient, k_band, preferred_element_type=jnp.float32
            ).astype(jnp.bfloat16)
        )
        dk_part = jnp.einsum(
            "kgqs,qkgd->skd", score_gradient, q_blk, preferred_element_type=jnp.float32
        )
        dv_part = jnp.einsum(
            "kgqs,qkgd->skd",
            attn_prob.astype(jnp.bfloat16),
            g_blk,
            preferred_element_type=jnp.float32,
        )
        for j in range(k_start // blk, k_end // blk):
            lo = j * blk - k_start
            for acc, part in ((dk_blocks, dk_part), (dv_blocks, dv_part)):
                piece = part[lo : lo + blk]
                acc[j] = piece if acc[j] is None else acc[j] + piece
    y_out = jnp.sum(pieces.astype(jnp.float32), axis=0).astype(jnp.bfloat16)
    dq_all = jnp.concatenate(dq_blocks, axis=0).reshape(win_rows, hq, HEAD_SIZE)
    dk_all = jnp.concatenate(dk_blocks, axis=0).astype(jnp.bfloat16)
    dv_all = jnp.concatenate(dv_blocks, axis=0).astype(jnp.bfloat16)
    packed_out = jnp.concatenate([dq_all, dk_all, dv_all], axis=1).reshape(
        seq_count, tok, hq + 2 * hk, HEAD_SIZE
    )
    back = lax.all_to_all(packed_out, SEQ, split_axis=0, concat_axis=0, tiled=True)
    back = back.transpose(1, 0, 2, 3)
    d_q = back[:, :, :hq].reshape(1, tok, QUERY_HEADS * HEAD_SIZE)
    key_gradient = back[:, :, hq : hq + hk].reshape(1, tok, KEY_VALUE_HEADS * HEAD_SIZE)
    value_gradient = back[:, :, hq + hk :].reshape(1, tok, KEY_VALUE_HEADS * HEAD_SIZE)
    y_count = lax.psum(1, "dpy")
    z_count = lax.psum(1, "dpz")
    cols = wo_grad.shape[1]
    wo_perm = (
        wo_grad.reshape(wo_grad.shape[0], y_count, z_count, cols // (y_count * z_count))
        .transpose(0, 2, 1, 3)
        .reshape(wo_grad.shape[0], cols)
    )
    wo_perm = lax.psum_scatter(wo_perm, "dpz", scatter_dimension=1, tiled=True)
    weight_grad = lax.psum_scatter(wo_perm, "dpy", scatter_dimension=1, tiled=True)
    return (
        y_out.reshape(1, tok, y_out.shape[1]),
        d_q,
        key_gradient,
        value_gradient,
        weight_grad,
    )


def solution(mesh):
    dp_count = mesh.shape["dp"]
    y_count = 4 if dp_count % 4 == 0 else 1
    seq_count = mesh.shape["seq"]
    core_count = 2 if seq_count % 2 == 0 else 1
    mesh = Mesh(
        mesh.devices.reshape(
            seq_count // core_count, core_count, y_count, dp_count // y_count
        ),
        ("x", "core", "dpy", "dpz"),
    )
    in_specs = (
        P(DP, SEQ, None),
        P(DP, SEQ, None),
        P(DP, SEQ, None),
        P(SEQ, None),
        P(DP, SEQ, None),
        P(DP, None),
        P(DP, None),
    )
    out_specs = (
        P(DP, SEQ, None),
        P(DP, SEQ, None),
        P(DP, SEQ, None),
        P(DP, SEQ, None),
        P(SEQ, DP),
    )
    return jax.shard_map(local, mesh=mesh, in_specs=in_specs, out_specs=out_specs, check_vma=False)
```

```python
import jax
import jax.numpy as jnp
from jax import lax
from jax.sharding import Mesh, PartitionSpec as P

QUERY_HEADS = 32
KEY_VALUE_HEADS = 8
HEAD_SIZE = 128
DP = ("dpy", "dpz")
SEQ = ("x", "core")
BLOCK = 256
MOST = 256


def row_starts(lengths, pack_order, win_rows):
    samples = lengths.shape[0]
    picked = jnp.sum(
        jnp.where(
            pack_order[:, None] == jnp.arange(samples, dtype=jnp.int32)[None, :],
            lengths[None, :],
            0,
        ),
        axis=1,
        dtype=jnp.int32,
    )
    seg_ends = jnp.cumsum(picked, dtype=jnp.int32)
    places = jnp.arange(win_rows, dtype=jnp.int32)
    return jnp.sum(
        jnp.where(seg_ends[None, :] <= places[:, None], picked[None, :], 0), axis=1, dtype=jnp.int32
    )


def local(queries, rotated_key_matrix, value_matrix, out_weight, out_grad, lengths, pack_order):
    seq_count = lax.psum(1, SEQ)
    x_count = lax.psum(1, "x")
    core_count = lax.psum(1, "core")
    tok = queries.shape[1]
    head_scale = HEAD_SIZE ** (-0.5)
    hq = QUERY_HEADS // seq_count
    hk = KEY_VALUE_HEADS // seq_count
    group_width = hq // hk
    packed = jnp.concatenate(
        [
            queries.reshape(tok, seq_count, hq, HEAD_SIZE),
            rotated_key_matrix.reshape(tok, seq_count, hk, HEAD_SIZE),
            value_matrix.reshape(tok, seq_count, hk, HEAD_SIZE),
        ],
        axis=2,
    ).transpose(1, 0, 2, 3)
    got = lax.all_to_all(packed, SEQ, split_axis=0, concat_axis=0, tiled=True)
    win_rows = seq_count * tok
    got = got.reshape(win_rows, hq + 2 * hk, HEAD_SIZE)
    query_head_rows = got[:, :hq].reshape(win_rows, hk, group_width, HEAD_SIZE)
    k_loc = got[:, hq : hq + hk]
    v_loc = got[:, hq + hk :]
    starts = row_starts(lengths[0], pack_order[0], win_rows)
    blk = min(BLOCK, win_rows)
    blk_count = win_rows // blk
    reach = -(-(MOST - 1) // blk)

    def band(i):
        q_start = i * blk
        k_start = max(0, q_start - reach * blk)
        return q_start, k_start, q_start + blk

    def probs(i, q_blk, m=None, l=None):
        q_start, k_start, k_end = band(i)
        k_band = k_loc[k_start:k_end]
        scores = (
            jnp.einsum("qkgd,skd->kgqs", q_blk, k_band, preferred_element_type=jnp.float32)
            * head_scale
        )
        rows_at = q_start + jnp.arange(blk, dtype=jnp.int32)
        cols_at = k_start + jnp.arange(k_end - k_start, dtype=jnp.int32)
        first_at = starts[q_start : q_start + blk]
        visible = (cols_at[None, :] >= first_at[:, None]) & (cols_at[None, :] <= rows_at[:, None])
        if m is None:
            m = jnp.max(jnp.where(visible, scores, -1e30), axis=-1, keepdims=True)
        expd = jnp.where(visible, jnp.exp(scores - m), 0.0)
        if l is None:
            l = jnp.sum(expd, axis=-1, keepdims=True)
        return expd / l, m, l

    out_blocks, stats = [], []
    for i in range(blk_count):
        q_start, k_start, k_end = band(i)
        q_blk = query_head_rows[q_start : q_start + blk]
        attn_prob, m, l = probs(i, q_blk)
        stats.append((m, l))
        out_blocks.append(
            jnp.einsum(
                "kgqs,skd->qkgd",
                attn_prob.astype(jnp.bfloat16),
                v_loc[k_start:k_end],
                preferred_element_type=jnp.float32,
            ).astype(jnp.bfloat16)
        )
    attn_out = jnp.concatenate(out_blocks, axis=0)
    a_head = attn_out.reshape(win_rows, hq * HEAD_SIZE)
    product = jnp.dot(a_head, out_weight, preferred_element_type=jnp.float32)
    pieces = (
        product.astype(jnp.bfloat16)
        .reshape(x_count, core_count, tok, product.shape[1])
        .transpose(1, 0, 2, 3)
    )
    g_mine = lax.all_gather(out_grad.reshape(tok, out_grad.shape[2]), "x", axis=0, tiled=False)
    g_other = lax.ppermute(
        g_mine, "core", perm=[(c, (c + 1) % core_count) for c in range(core_count)]
    )
    core_at = lax.axis_index("core")
    a_split = a_head.reshape(x_count, core_count, tok, hq * HEAD_SIZE)
    a_mine = lax.dynamic_index_in_dim(a_split, core_at, axis=1, keepdims=False)
    a_other = lax.dynamic_index_in_dim(a_split, 1 - core_at, axis=1, keepdims=False)
    contract_rows = (((0, 1), (0, 1)), ((), ()))
    wo_grad = lax.dot_general(
        a_mine, g_mine, contract_rows, preferred_element_type=jnp.float32
    ) + lax.dot_general(a_other, g_other, contract_rows, preferred_element_type=jnp.float32)
    contract_cols = (((2,), (1,)), ((), ()))
    d_mine = lax.dot_general(
        g_mine, out_weight, contract_cols, preferred_element_type=jnp.float32
    ).astype(jnp.bfloat16)
    d_other = lax.dot_general(
        g_other, out_weight, contract_cols, preferred_element_type=jnp.float32
    ).astype(jnp.bfloat16)
    d_rows = jnp.where(
        core_at == 0,
        jnp.stack([d_mine, d_other], axis=1),
        jnp.stack([d_other, d_mine], axis=1),
    )
    attention_grad = d_rows.reshape(win_rows, hk, group_width, HEAD_SIZE)
    pieces, attention_grad = lax.optimization_barrier((pieces, attention_grad))
    pieces = lax.all_to_all(pieces, "core", split_axis=0, concat_axis=0, tiled=True)
    pieces = jnp.sum(pieces.astype(jnp.float32), axis=0).astype(jnp.bfloat16)
    pieces = lax.all_to_all(pieces, "x", split_axis=0, concat_axis=0, tiled=True)

    dq_blocks = []
    dk_blocks = [None] * blk_count
    dv_blocks = [None] * blk_count
    for i in range(blk_count):
        if i == blk_count // 2:
            pieces, attention_grad = lax.optimization_barrier((pieces, attention_grad))
        q_start, k_start, k_end = band(i)
        q_blk = query_head_rows[q_start : q_start + blk]
        g_blk = attention_grad[q_start : q_start + blk]
        o_blk = attn_out[q_start : q_start + blk]
        row_dot = jnp.sum(g_blk.astype(jnp.float32) * o_blk.astype(jnp.float32), axis=-1)
        row_dot = jnp.transpose(row_dot, (1, 2, 0))[..., None]
        attn_prob, _, _ = probs(i, q_blk, *stats[i])
        k_band = k_loc[k_start:k_end]
        v_band = v_loc[k_start:k_end]
        d_prob = jnp.einsum("qkgd,skd->kgqs", g_blk, v_band, preferred_element_type=jnp.float32)
        score_gradient = (attn_prob * (d_prob - row_dot) * head_scale).astype(jnp.bfloat16)
        dq_blocks.append(
            jnp.einsum(
                "kgqs,skd->qkgd", score_gradient, k_band, preferred_element_type=jnp.float32
            ).astype(jnp.bfloat16)
        )
        dk_part = jnp.einsum(
            "kgqs,qkgd->skd", score_gradient, q_blk, preferred_element_type=jnp.float32
        )
        dv_part = jnp.einsum(
            "kgqs,qkgd->skd",
            attn_prob.astype(jnp.bfloat16),
            g_blk,
            preferred_element_type=jnp.float32,
        )
        for j in range(k_start // blk, k_end // blk):
            lo = j * blk - k_start
            for acc, part in ((dk_blocks, dk_part), (dv_blocks, dv_part)):
                piece = part[lo : lo + blk]
                acc[j] = piece if acc[j] is None else acc[j] + piece
    y_out = jnp.sum(pieces.astype(jnp.float32), axis=0).astype(jnp.bfloat16)
    dq_all = jnp.concatenate(dq_blocks, axis=0).reshape(win_rows, hq, HEAD_SIZE)
    dk_all = jnp.concatenate(dk_blocks, axis=0).astype(jnp.bfloat16)
    dv_all = jnp.concatenate(dv_blocks, axis=0).astype(jnp.bfloat16)
    packed_out = jnp.concatenate([dq_all, dk_all, dv_all], axis=1).reshape(
        seq_count, tok, hq + 2 * hk, HEAD_SIZE
    )
    back = lax.all_to_all(packed_out, SEQ, split_axis=0, concat_axis=0, tiled=True)
    back = back.transpose(1, 0, 2, 3)
    d_q = back[:, :, :hq].reshape(1, tok, QUERY_HEADS * HEAD_SIZE)
    key_gradient = back[:, :, hq : hq + hk].reshape(1, tok, KEY_VALUE_HEADS * HEAD_SIZE)
    value_gradient = back[:, :, hq + hk :].reshape(1, tok, KEY_VALUE_HEADS * HEAD_SIZE)
    y_count = lax.psum(1, "dpy")
    z_count = lax.psum(1, "dpz")
    cols = wo_grad.shape[1]
    wo_perm = (
        wo_grad.reshape(wo_grad.shape[0], y_count, z_count, cols // (y_count * z_count))
        .transpose(0, 2, 1, 3)
        .reshape(wo_grad.shape[0], cols)
    )
    wo_perm = lax.psum_scatter(wo_perm, "dpz", scatter_dimension=1, tiled=True)
    weight_grad = lax.psum_scatter(wo_perm, "dpy", scatter_dimension=1, tiled=True)
    return (
        y_out.reshape(1, tok, y_out.shape[1]),
        d_q,
        key_gradient,
        value_gradient,
        weight_grad,
    )


def solution(mesh):
    dp_count = mesh.shape["dp"]
    y_count = 4 if dp_count % 4 == 0 else 1
    seq_count = mesh.shape["seq"]
    core_count = 2 if seq_count % 2 == 0 else 1
    mesh = Mesh(
        mesh.devices.reshape(
            seq_count // core_count, core_count, y_count, dp_count // y_count
        ),
        ("x", "core", "dpy", "dpz"),
    )
    in_specs = (
        P(DP, SEQ, None),
        P(DP, SEQ, None),
        P(DP, SEQ, None),
        P(SEQ, None),
        P(DP, SEQ, None),
        P(DP, None),
        P(DP, None),
    )
    out_specs = (
        P(DP, SEQ, None),
        P(DP, SEQ, None),
        P(DP, SEQ, None),
        P(DP, SEQ, None),
        P(SEQ, DP),
    )
    return jax.shard_map(local, mesh=mesh, in_specs=in_specs, out_specs=out_specs, check_vma=False)
```

```python
import jax
import jax.numpy as jnp
from jax import lax
from jax.sharding import Mesh, PartitionSpec as P

QUERY_HEADS = 32
KEY_VALUE_HEADS = 8
HEAD_SIZE = 128
DP = ("dpy", "dpz")
SEQ = ("x", "core")
BLOCK = 256
MOST = 256


def row_starts(lengths, pack_order, win_rows):
    samples = lengths.shape[0]
    picked = jnp.sum(
        jnp.where(
            pack_order[:, None] == jnp.arange(samples, dtype=jnp.int32)[None, :],
            lengths[None, :],
            0,
        ),
        axis=1,
        dtype=jnp.int32,
    )
    seg_ends = jnp.cumsum(picked, dtype=jnp.int32)
    places = jnp.arange(win_rows, dtype=jnp.int32)
    return jnp.sum(
        jnp.where(seg_ends[None, :] <= places[:, None], picked[None, :], 0), axis=1, dtype=jnp.int32
    )


def local(queries, rotated_key_matrix, value_matrix, out_weight, out_grad, lengths, pack_order):
    seq_count = lax.psum(1, SEQ)
    x_count = lax.psum(1, "x")
    core_count = lax.psum(1, "core")
    tok = queries.shape[1]
    head_scale = HEAD_SIZE ** (-0.5)
    hq = QUERY_HEADS // seq_count
    hk = KEY_VALUE_HEADS // seq_count
    group_width = hq // hk
    packed = jnp.concatenate(
        [
            queries.reshape(tok, seq_count, hq, HEAD_SIZE),
            rotated_key_matrix.reshape(tok, seq_count, hk, HEAD_SIZE),
            value_matrix.reshape(tok, seq_count, hk, HEAD_SIZE),
        ],
        axis=2,
    ).transpose(1, 0, 2, 3)
    got = lax.all_to_all(packed, SEQ, split_axis=0, concat_axis=0, tiled=True)
    win_rows = seq_count * tok
    got = got.reshape(win_rows, hq + 2 * hk, HEAD_SIZE)
    query_head_rows = got[:, :hq].reshape(win_rows, hk, group_width, HEAD_SIZE)
    k_loc = got[:, hq : hq + hk]
    v_loc = got[:, hq + hk :]
    starts = row_starts(lengths[0], pack_order[0], win_rows)
    blk = min(BLOCK, win_rows)
    blk_count = win_rows // blk
    reach = -(-(MOST - 1) // blk)

    def band(i):
        q_start = i * blk
        k_start = max(0, q_start - reach * blk)
        return q_start, k_start, q_start + blk

    def probs(i, q_blk, m=None, l=None):
        q_start, k_start, k_end = band(i)
        k_band = k_loc[k_start:k_end]
        scores = (
            jnp.einsum("qkgd,skd->kgqs", q_blk, k_band, preferred_element_type=jnp.float32)
            * head_scale
        )
        rows_at = q_start + jnp.arange(blk, dtype=jnp.int32)
        cols_at = k_start + jnp.arange(k_end - k_start, dtype=jnp.int32)
        first_at = starts[q_start : q_start + blk]
        visible = (cols_at[None, :] >= first_at[:, None]) & (cols_at[None, :] <= rows_at[:, None])
        if m is None:
            m = jnp.max(jnp.where(visible, scores, -1e30), axis=-1, keepdims=True)
        expd = jnp.where(visible, jnp.exp(scores - m), 0.0)
        if l is None:
            l = jnp.sum(expd, axis=-1, keepdims=True)
        return expd / l, m, l

    out_blocks, stats = [], []
    for i in range(blk_count):
        q_start, k_start, k_end = band(i)
        q_blk = query_head_rows[q_start : q_start + blk]
        attn_prob, m, l = probs(i, q_blk)
        stats.append((m, l))
        out_blocks.append(
            jnp.einsum(
                "kgqs,skd->qkgd",
                attn_prob.astype(jnp.bfloat16),
                v_loc[k_start:k_end],
                preferred_element_type=jnp.float32,
            ).astype(jnp.bfloat16)
        )
    attn_out = jnp.concatenate(out_blocks, axis=0)
    a_head = attn_out.reshape(win_rows, hq * HEAD_SIZE)
    product = jnp.dot(a_head, out_weight, preferred_element_type=jnp.float32)
    pieces = (
        product.astype(jnp.bfloat16)
        .reshape(x_count, core_count, tok, product.shape[1])
        .transpose(1, 0, 2, 3)
    )
    g_mine = lax.all_gather(out_grad.reshape(tok, out_grad.shape[2]), "x", axis=0, tiled=False)
    g_other = lax.ppermute(
        g_mine, "core", perm=[(c, (c + 1) % core_count) for c in range(core_count)]
    )
    core_at = lax.axis_index("core")
    incoming = jnp.where(
        core_at == 0,
        jnp.stack([g_mine, g_other], axis=1),
        jnp.stack([g_other, g_mine], axis=1),
    ).reshape(win_rows, g_mine.shape[2])
    wo_grad = lax.dot_general(
        a_head, incoming, (((0,), (0,)), ((), ())), preferred_element_type=jnp.float32
    )
    d_rows = lax.dot_general(
        incoming, out_weight, (((1,), (1,)), ((), ())), preferred_element_type=jnp.float32
    ).astype(jnp.bfloat16)
    attention_grad = d_rows.reshape(win_rows, hk, group_width, HEAD_SIZE)
    pieces, attention_grad = lax.optimization_barrier((pieces, attention_grad))
    pieces = lax.all_to_all(pieces, "core", split_axis=0, concat_axis=0, tiled=True)
    pieces = jnp.sum(pieces.astype(jnp.float32), axis=0).astype(jnp.bfloat16)
    pieces = lax.all_to_all(pieces, "x", split_axis=0, concat_axis=0, tiled=True)

    dq_blocks = []
    dk_blocks = [None] * blk_count
    dv_blocks = [None] * blk_count
    for i in range(blk_count):
        if i == blk_count // 2:
            pieces, attention_grad = lax.optimization_barrier((pieces, attention_grad))
        q_start, k_start, k_end = band(i)
        q_blk = query_head_rows[q_start : q_start + blk]
        g_blk = attention_grad[q_start : q_start + blk]
        o_blk = attn_out[q_start : q_start + blk]
        row_dot = jnp.sum(g_blk.astype(jnp.float32) * o_blk.astype(jnp.float32), axis=-1)
        row_dot = jnp.transpose(row_dot, (1, 2, 0))[..., None]
        attn_prob, _, _ = probs(i, q_blk, *stats[i])
        k_band = k_loc[k_start:k_end]
        v_band = v_loc[k_start:k_end]
        d_prob = jnp.einsum("qkgd,skd->kgqs", g_blk, v_band, preferred_element_type=jnp.float32)
        score_gradient = (attn_prob * (d_prob - row_dot) * head_scale).astype(jnp.bfloat16)
        dq_blocks.append(
            jnp.einsum(
                "kgqs,skd->qkgd", score_gradient, k_band, preferred_element_type=jnp.float32
            ).astype(jnp.bfloat16)
        )
        dk_part = jnp.einsum(
            "kgqs,qkgd->skd", score_gradient, q_blk, preferred_element_type=jnp.float32
        )
        dv_part = jnp.einsum(
            "kgqs,qkgd->skd",
            attn_prob.astype(jnp.bfloat16),
            g_blk,
            preferred_element_type=jnp.float32,
        )
        for j in range(k_start // blk, k_end // blk):
            lo = j * blk - k_start
            for acc, part in ((dk_blocks, dk_part), (dv_blocks, dv_part)):
                piece = part[lo : lo + blk]
                acc[j] = piece if acc[j] is None else acc[j] + piece
    y_out = jnp.sum(pieces.astype(jnp.float32), axis=0).astype(jnp.bfloat16)
    dq_all = jnp.concatenate(dq_blocks, axis=0).reshape(win_rows, hq, HEAD_SIZE)
    dk_all = jnp.concatenate(dk_blocks, axis=0).astype(jnp.bfloat16)
    dv_all = jnp.concatenate(dv_blocks, axis=0).astype(jnp.bfloat16)
    packed_out = jnp.concatenate([dq_all, dk_all, dv_all], axis=1).reshape(
        seq_count, tok, hq + 2 * hk, HEAD_SIZE
    )
    back = lax.all_to_all(packed_out, SEQ, split_axis=0, concat_axis=0, tiled=True)
    back = back.transpose(1, 0, 2, 3)
    d_q = back[:, :, :hq].reshape(1, tok, QUERY_HEADS * HEAD_SIZE)
    key_gradient = back[:, :, hq : hq + hk].reshape(1, tok, KEY_VALUE_HEADS * HEAD_SIZE)
    value_gradient = back[:, :, hq + hk :].reshape(1, tok, KEY_VALUE_HEADS * HEAD_SIZE)
    y_count = lax.psum(1, "dpy")
    z_count = lax.psum(1, "dpz")
    cols = wo_grad.shape[1]
    wo_perm = (
        wo_grad.reshape(wo_grad.shape[0], y_count, z_count, cols // (y_count * z_count))
        .transpose(0, 2, 1, 3)
        .reshape(wo_grad.shape[0], cols)
    )
    wo_perm = lax.psum_scatter(wo_perm, "dpz", scatter_dimension=1, tiled=True)
    weight_grad = lax.psum_scatter(wo_perm, "dpy", scatter_dimension=1, tiled=True)
    return (
        y_out.reshape(1, tok, y_out.shape[1]),
        d_q,
        key_gradient,
        value_gradient,
        weight_grad,
    )


def solution(mesh):
    dp_count = mesh.shape["dp"]
    y_count = 4 if dp_count % 4 == 0 else 1
    seq_count = mesh.shape["seq"]
    core_count = 2 if seq_count % 2 == 0 else 1
    mesh = Mesh(
        mesh.devices.reshape(
            seq_count // core_count, core_count, y_count, dp_count // y_count
        ),
        ("x", "core", "dpy", "dpz"),
    )
    in_specs = (
        P(DP, SEQ, None),
        P(DP, SEQ, None),
        P(DP, SEQ, None),
        P(SEQ, None),
        P(DP, SEQ, None),
        P(DP, None),
        P(DP, None),
    )
    out_specs = (
        P(DP, SEQ, None),
        P(DP, SEQ, None),
        P(DP, SEQ, None),
        P(DP, SEQ, None),
        P(SEQ, DP),
    )
    return jax.shard_map(local, mesh=mesh, in_specs=in_specs, out_specs=out_specs, check_vma=False)
```

```python
import jax
import jax.numpy as jnp
from jax import lax
from jax.sharding import Mesh, PartitionSpec as P

QUERY_HEADS = 32
KEY_VALUE_HEADS = 8
HEAD_SIZE = 128
DP = ("dpy", "dpz")
SEQ = ("x", "core")
BLOCK = 256
MOST = 256


def row_starts(lengths, pack_order, win_rows):
    samples = lengths.shape[0]
    picked = jnp.sum(
        jnp.where(
            pack_order[:, None] == jnp.arange(samples, dtype=jnp.int32)[None, :],
            lengths[None, :],
            0,
        ),
        axis=1,
        dtype=jnp.int32,
    )
    seg_ends = jnp.cumsum(picked, dtype=jnp.int32)
    places = jnp.arange(win_rows, dtype=jnp.int32)
    return jnp.sum(
        jnp.where(seg_ends[None, :] <= places[:, None], picked[None, :], 0), axis=1, dtype=jnp.int32
    )


def local(queries, rotated_key_matrix, value_matrix, out_weight, out_grad, lengths, pack_order):
    seq_count = lax.psum(1, SEQ)
    x_count = lax.psum(1, "x")
    core_count = lax.psum(1, "core")
    tok = queries.shape[1]
    head_scale = HEAD_SIZE ** (-0.5)
    hq = QUERY_HEADS // seq_count
    hk = KEY_VALUE_HEADS // seq_count
    group_width = hq // hk
    packed = jnp.concatenate(
        [
            queries.reshape(tok, seq_count, hq, HEAD_SIZE),
            rotated_key_matrix.reshape(tok, seq_count, hk, HEAD_SIZE),
            value_matrix.reshape(tok, seq_count, hk, HEAD_SIZE),
        ],
        axis=2,
    ).transpose(1, 0, 2, 3)
    got = lax.all_to_all(packed, SEQ, split_axis=0, concat_axis=0, tiled=True)
    got, out_grad = lax.optimization_barrier((got, out_grad))
    win_rows = seq_count * tok
    got = got.reshape(win_rows, hq + 2 * hk, HEAD_SIZE)
    query_head_rows = got[:, :hq].reshape(win_rows, hk, group_width, HEAD_SIZE)
    k_loc = got[:, hq : hq + hk]
    v_loc = got[:, hq + hk :]
    starts = row_starts(lengths[0], pack_order[0], win_rows)
    blk = min(BLOCK, win_rows)
    blk_count = win_rows // blk
    reach = -(-(MOST - 1) // blk)

    def band(i):
        q_start = i * blk
        k_start = max(0, q_start - reach * blk)
        return q_start, k_start, q_start + blk

    def probs(i, q_blk, m=None, l=None):
        q_start, k_start, k_end = band(i)
        k_band = k_loc[k_start:k_end]
        scores = (
            jnp.einsum("qkgd,skd->kgqs", q_blk, k_band, preferred_element_type=jnp.float32)
            * head_scale
        )
        rows_at = q_start + jnp.arange(blk, dtype=jnp.int32)
        cols_at = k_start + jnp.arange(k_end - k_start, dtype=jnp.int32)
        first_at = starts[q_start : q_start + blk]
        visible = (cols_at[None, :] >= first_at[:, None]) & (cols_at[None, :] <= rows_at[:, None])
        if m is None:
            m = jnp.max(jnp.where(visible, scores, -1e30), axis=-1, keepdims=True)
        expd = jnp.where(visible, jnp.exp(scores - m), 0.0)
        if l is None:
            l = jnp.sum(expd, axis=-1, keepdims=True)
        return expd / l, m, l

    out_blocks, stats = [], []
    for i in range(blk_count):
        q_start, k_start, k_end = band(i)
        q_blk = query_head_rows[q_start : q_start + blk]
        attn_prob, m, l = probs(i, q_blk)
        stats.append((m, l))
        out_blocks.append(
            jnp.einsum(
                "kgqs,skd->qkgd",
                attn_prob.astype(jnp.bfloat16),
                v_loc[k_start:k_end],
                preferred_element_type=jnp.float32,
            ).astype(jnp.bfloat16)
        )
    attn_out = jnp.concatenate(out_blocks, axis=0)
    a_head = attn_out.reshape(win_rows, hq * HEAD_SIZE)
    product = jnp.dot(a_head, out_weight, preferred_element_type=jnp.float32)
    pieces = (
        product.astype(jnp.bfloat16)
        .reshape(x_count, core_count, tok, product.shape[1])
        .transpose(1, 0, 2, 3)
    )
    g_mine = lax.all_gather(out_grad.reshape(tok, out_grad.shape[2]), "x", axis=0, tiled=False)
    g_other = lax.ppermute(
        g_mine, "core", perm=[(c, (c + 1) % core_count) for c in range(core_count)]
    )
    core_at = lax.axis_index("core")
    incoming = jnp.where(
        core_at == 0,
        jnp.stack([g_mine, g_other], axis=1),
        jnp.stack([g_other, g_mine], axis=1),
    ).reshape(win_rows, g_mine.shape[2])
    wo_grad = lax.dot_general(
        a_head, incoming, (((0,), (0,)), ((), ())), preferred_element_type=jnp.float32
    )
    d_rows = lax.dot_general(
        incoming, out_weight, (((1,), (1,)), ((), ())), preferred_element_type=jnp.float32
    ).astype(jnp.bfloat16)
    attention_grad = d_rows.reshape(win_rows, hk, group_width, HEAD_SIZE)
    pieces, attention_grad = lax.optimization_barrier((pieces, attention_grad))
    pieces = lax.all_to_all(pieces, "core", split_axis=0, concat_axis=0, tiled=True)
    pieces = jnp.sum(pieces.astype(jnp.float32), axis=0).astype(jnp.bfloat16)
    pieces = lax.all_to_all(pieces, "x", split_axis=0, concat_axis=0, tiled=True)

    dq_blocks = []
    dk_blocks = [None] * blk_count
    dv_blocks = [None] * blk_count
    for i in range(blk_count):
        if i == blk_count // 2:
            pieces, attention_grad = lax.optimization_barrier((pieces, attention_grad))
        q_start, k_start, k_end = band(i)
        q_blk = query_head_rows[q_start : q_start + blk]
        g_blk = attention_grad[q_start : q_start + blk]
        o_blk = attn_out[q_start : q_start + blk]
        row_dot = jnp.sum(g_blk.astype(jnp.float32) * o_blk.astype(jnp.float32), axis=-1)
        row_dot = jnp.transpose(row_dot, (1, 2, 0))[..., None]
        attn_prob, _, _ = probs(i, q_blk, *stats[i])
        k_band = k_loc[k_start:k_end]
        v_band = v_loc[k_start:k_end]
        d_prob = jnp.einsum("qkgd,skd->kgqs", g_blk, v_band, preferred_element_type=jnp.float32)
        score_gradient = (attn_prob * (d_prob - row_dot) * head_scale).astype(jnp.bfloat16)
        dq_blocks.append(
            jnp.einsum(
                "kgqs,skd->qkgd", score_gradient, k_band, preferred_element_type=jnp.float32
            ).astype(jnp.bfloat16)
        )
        dk_part = jnp.einsum(
            "kgqs,qkgd->skd", score_gradient, q_blk, preferred_element_type=jnp.float32
        )
        dv_part = jnp.einsum(
            "kgqs,qkgd->skd",
            attn_prob.astype(jnp.bfloat16),
            g_blk,
            preferred_element_type=jnp.float32,
        )
        for j in range(k_start // blk, k_end // blk):
            lo = j * blk - k_start
            for acc, part in ((dk_blocks, dk_part), (dv_blocks, dv_part)):
                piece = part[lo : lo + blk]
                acc[j] = piece if acc[j] is None else acc[j] + piece
    y_out = jnp.sum(pieces.astype(jnp.float32), axis=0).astype(jnp.bfloat16)
    dq_all = jnp.concatenate(dq_blocks, axis=0).reshape(win_rows, hq, HEAD_SIZE)
    dk_all = jnp.concatenate(dk_blocks, axis=0).astype(jnp.bfloat16)
    dv_all = jnp.concatenate(dv_blocks, axis=0).astype(jnp.bfloat16)
    packed_out = jnp.concatenate([dq_all, dk_all, dv_all], axis=1).reshape(
        seq_count, tok, hq + 2 * hk, HEAD_SIZE
    )
    back = lax.all_to_all(packed_out, SEQ, split_axis=0, concat_axis=0, tiled=True)
    back = back.transpose(1, 0, 2, 3)
    d_q = back[:, :, :hq].reshape(1, tok, QUERY_HEADS * HEAD_SIZE)
    key_gradient = back[:, :, hq : hq + hk].reshape(1, tok, KEY_VALUE_HEADS * HEAD_SIZE)
    value_gradient = back[:, :, hq + hk :].reshape(1, tok, KEY_VALUE_HEADS * HEAD_SIZE)
    y_count = lax.psum(1, "dpy")
    z_count = lax.psum(1, "dpz")
    cols = wo_grad.shape[1]
    wo_perm = (
        wo_grad.reshape(wo_grad.shape[0], y_count, z_count, cols // (y_count * z_count))
        .transpose(0, 2, 1, 3)
        .reshape(wo_grad.shape[0], cols)
    )
    wo_perm = lax.psum_scatter(wo_perm, "dpz", scatter_dimension=1, tiled=True)
    weight_grad = lax.psum_scatter(wo_perm, "dpy", scatter_dimension=1, tiled=True)
    return (
        y_out.reshape(1, tok, y_out.shape[1]),
        d_q,
        key_gradient,
        value_gradient,
        weight_grad,
    )


def solution(mesh):
    dp_count = mesh.shape["dp"]
    y_count = 4 if dp_count % 4 == 0 else 1
    seq_count = mesh.shape["seq"]
    core_count = 2 if seq_count % 2 == 0 else 1
    mesh = Mesh(
        mesh.devices.reshape(
            seq_count // core_count, core_count, y_count, dp_count // y_count
        ),
        ("x", "core", "dpy", "dpz"),
    )
    in_specs = (
        P(DP, SEQ, None),
        P(DP, SEQ, None),
        P(DP, SEQ, None),
        P(SEQ, None),
        P(DP, SEQ, None),
        P(DP, None),
        P(DP, None),
    )
    out_specs = (
        P(DP, SEQ, None),
        P(DP, SEQ, None),
        P(DP, SEQ, None),
        P(DP, SEQ, None),
        P(SEQ, DP),
    )
    return jax.shard_map(local, mesh=mesh, in_specs=in_specs, out_specs=out_specs, check_vma=False)
```

```python
import jax
import jax.numpy as jnp
from jax import lax
from jax.sharding import Mesh, PartitionSpec as P

QUERY_HEADS = 32
KEY_VALUE_HEADS = 8
HEAD_SIZE = 128
DP = ("dpy", "dpz")
SEQ = ("x", "core")
BLOCK = 256
MOST = 256


def row_starts(lengths, pack_order, win_rows):
    samples = lengths.shape[0]
    picked = jnp.sum(
        jnp.where(
            pack_order[:, None] == jnp.arange(samples, dtype=jnp.int32)[None, :],
            lengths[None, :],
            0,
        ),
        axis=1,
        dtype=jnp.int32,
    )
    seg_ends = jnp.cumsum(picked, dtype=jnp.int32)
    places = jnp.arange(win_rows, dtype=jnp.int32)
    return jnp.sum(
        jnp.where(seg_ends[None, :] <= places[:, None], picked[None, :], 0), axis=1, dtype=jnp.int32
    )


def local(queries, rotated_key_matrix, value_matrix, out_weight, out_grad, lengths, pack_order):
    seq_count = lax.psum(1, SEQ)
    x_count = lax.psum(1, "x")
    core_count = lax.psum(1, "core")
    tok = queries.shape[1]
    head_scale = HEAD_SIZE ** (-0.5)
    hq = QUERY_HEADS // seq_count
    hk = KEY_VALUE_HEADS // seq_count
    group_width = hq // hk
    packed = jnp.concatenate(
        [
            queries.reshape(tok, seq_count, hq, HEAD_SIZE),
            rotated_key_matrix.reshape(tok, seq_count, hk, HEAD_SIZE),
            value_matrix.reshape(tok, seq_count, hk, HEAD_SIZE),
        ],
        axis=2,
    ).transpose(1, 0, 2, 3)
    got = lax.all_to_all(packed, SEQ, split_axis=0, concat_axis=0, tiled=True)
    win_rows = seq_count * tok
    got = got.reshape(win_rows, hq + 2 * hk, HEAD_SIZE)
    query_head_rows = got[:, :hq].reshape(win_rows, hk, group_width, HEAD_SIZE)
    k_loc = got[:, hq : hq + hk]
    v_loc = got[:, hq + hk :]
    starts = row_starts(lengths[0], pack_order[0], win_rows)
    blk = min(BLOCK, win_rows)
    blk_count = win_rows // blk
    reach = -(-(MOST - 1) // blk)

    def band(i):
        q_start = i * blk
        k_start = max(0, q_start - reach * blk)
        return q_start, k_start, q_start + blk

    def probs(i, q_blk, m=None, l=None):
        q_start, k_start, k_end = band(i)
        k_band = k_loc[k_start:k_end]
        scores = (
            jnp.einsum("qkgd,skd->kgqs", q_blk, k_band, preferred_element_type=jnp.float32)
            * head_scale
        )
        rows_at = q_start + jnp.arange(blk, dtype=jnp.int32)
        cols_at = k_start + jnp.arange(k_end - k_start, dtype=jnp.int32)
        first_at = starts[q_start : q_start + blk]
        visible = (cols_at[None, :] >= first_at[:, None]) & (cols_at[None, :] <= rows_at[:, None])
        if m is None:
            m = jnp.max(jnp.where(visible, scores, -1e30), axis=-1, keepdims=True)
        expd = jnp.where(visible, jnp.exp(scores - m), 0.0)
        if l is None:
            l = jnp.sum(expd, axis=-1, keepdims=True)
        return expd / l, m, l

    out_blocks, stats = [], []
    for i in range(blk_count):
        q_start, k_start, k_end = band(i)
        q_blk = query_head_rows[q_start : q_start + blk]
        attn_prob, m, l = probs(i, q_blk)
        stats.append((m, l))
        out_blocks.append(
            jnp.einsum(
                "kgqs,skd->qkgd",
                attn_prob.astype(jnp.bfloat16),
                v_loc[k_start:k_end],
                preferred_element_type=jnp.float32,
            ).astype(jnp.bfloat16)
        )
    attn_out = jnp.concatenate(out_blocks, axis=0)
    a_head = attn_out.reshape(win_rows, hq * HEAD_SIZE)
    product = jnp.dot(a_head, out_weight, preferred_element_type=jnp.float32)
    pieces = (
        product.astype(jnp.bfloat16)
        .reshape(x_count, core_count, tok, product.shape[1])
        .transpose(1, 0, 2, 3)
    )
    incoming = lax.all_gather(out_grad.reshape(tok, out_grad.shape[2]), SEQ, axis=0, tiled=True)
    wo_grad = lax.dot_general(
        a_head, incoming, (((0,), (0,)), ((), ())), preferred_element_type=jnp.float32
    )
    d_rows = lax.dot_general(
        incoming, out_weight, (((1,), (1,)), ((), ())), preferred_element_type=jnp.float32
    )
    attention_grad = d_rows.astype(jnp.bfloat16).reshape(win_rows, hk, group_width, HEAD_SIZE)
    pieces, attention_grad = lax.optimization_barrier((pieces, attention_grad))
    pieces = lax.all_to_all(pieces, "core", split_axis=0, concat_axis=0, tiled=True)
    pieces = jnp.sum(pieces.astype(jnp.float32), axis=0).astype(jnp.bfloat16)
    pieces = lax.all_to_all(pieces, "x", split_axis=0, concat_axis=0, tiled=True)

    dq_blocks = []
    dk_blocks = [None] * blk_count
    dv_blocks = [None] * blk_count
    for i in range(blk_count):
        if i == blk_count - 1:
            pieces, attention_grad = lax.optimization_barrier((pieces, attention_grad))
        q_start, k_start, k_end = band(i)
        q_blk = query_head_rows[q_start : q_start + blk]
        g_blk = attention_grad[q_start : q_start + blk]
        o_blk = attn_out[q_start : q_start + blk]
        row_dot = jnp.sum(g_blk.astype(jnp.float32) * o_blk.astype(jnp.float32), axis=-1)
        row_dot = jnp.transpose(row_dot, (1, 2, 0))[..., None]
        attn_prob, _, _ = probs(i, q_blk, *stats[i])
        k_band = k_loc[k_start:k_end]
        v_band = v_loc[k_start:k_end]
        d_prob = jnp.einsum("qkgd,skd->kgqs", g_blk, v_band, preferred_element_type=jnp.float32)
        score_gradient = (attn_prob * (d_prob - row_dot) * head_scale).astype(jnp.bfloat16)
        dq_blocks.append(
            jnp.einsum(
                "kgqs,skd->qkgd", score_gradient, k_band, preferred_element_type=jnp.float32
            ).astype(jnp.bfloat16)
        )
        dk_part = jnp.einsum(
            "kgqs,qkgd->skd", score_gradient, q_blk, preferred_element_type=jnp.float32
        )
        dv_part = jnp.einsum(
            "kgqs,qkgd->skd",
            attn_prob.astype(jnp.bfloat16),
            g_blk,
            preferred_element_type=jnp.float32,
        )
        for j in range(k_start // blk, k_end // blk):
            lo = j * blk - k_start
            for acc, part in ((dk_blocks, dk_part), (dv_blocks, dv_part)):
                piece = part[lo : lo + blk]
                acc[j] = piece if acc[j] is None else acc[j] + piece
    y_out = jnp.sum(pieces.astype(jnp.float32), axis=0).astype(jnp.bfloat16)
    dq_all = jnp.concatenate(dq_blocks, axis=0).reshape(win_rows, hq, HEAD_SIZE)
    dk_all = jnp.concatenate(dk_blocks, axis=0).astype(jnp.bfloat16)
    dv_all = jnp.concatenate(dv_blocks, axis=0).astype(jnp.bfloat16)
    packed_out = jnp.concatenate([dq_all, dk_all, dv_all], axis=1).reshape(
        seq_count, tok, hq + 2 * hk, HEAD_SIZE
    )
    back = lax.all_to_all(packed_out, SEQ, split_axis=0, concat_axis=0, tiled=True)
    back = back.transpose(1, 0, 2, 3)
    d_q = back[:, :, :hq].reshape(1, tok, QUERY_HEADS * HEAD_SIZE)
    key_gradient = back[:, :, hq : hq + hk].reshape(1, tok, KEY_VALUE_HEADS * HEAD_SIZE)
    value_gradient = back[:, :, hq + hk :].reshape(1, tok, KEY_VALUE_HEADS * HEAD_SIZE)
    y_count = lax.psum(1, "dpy")
    z_count = lax.psum(1, "dpz")
    cols = wo_grad.shape[1]
    wo_perm = (
        wo_grad.reshape(wo_grad.shape[0], y_count, z_count, cols // (y_count * z_count))
        .transpose(0, 2, 1, 3)
        .reshape(wo_grad.shape[0], cols)
    )
    wo_perm = lax.psum_scatter(wo_perm, "dpz", scatter_dimension=1, tiled=True)
    weight_grad = lax.psum_scatter(wo_perm, "dpy", scatter_dimension=1, tiled=True)
    return (
        y_out.reshape(1, tok, y_out.shape[1]),
        d_q,
        key_gradient,
        value_gradient,
        weight_grad,
    )


def solution(mesh):
    dp_count = mesh.shape["dp"]
    y_count = 4 if dp_count % 4 == 0 else 1
    seq_count = mesh.shape["seq"]
    core_count = 2 if seq_count % 2 == 0 else 1
    mesh = Mesh(
        mesh.devices.reshape(
            seq_count // core_count, core_count, y_count, dp_count // y_count
        ),
        ("x", "core", "dpy", "dpz"),
    )
    in_specs = (
        P(DP, SEQ, None),
        P(DP, SEQ, None),
        P(DP, SEQ, None),
        P(SEQ, None),
        P(DP, SEQ, None),
        P(DP, None),
        P(DP, None),
    )
    out_specs = (
        P(DP, SEQ, None),
        P(DP, SEQ, None),
        P(DP, SEQ, None),
        P(DP, SEQ, None),
        P(SEQ, DP),
    )
    return jax.shard_map(local, mesh=mesh, in_specs=in_specs, out_specs=out_specs, check_vma=False)
```

```python
import jax
import jax.numpy as jnp
from jax import lax
from jax.sharding import Mesh, PartitionSpec as P

QUERY_HEADS = 32
KEY_VALUE_HEADS = 8
HEAD_SIZE = 128
DP = ("dpy", "dpz")
SEQ = ("x", "core")
BLOCK = 256
MOST = 256


def row_starts(lengths, pack_order, win_rows):
    samples = lengths.shape[0]
    picked = jnp.sum(
        jnp.where(
            pack_order[:, None] == jnp.arange(samples, dtype=jnp.int32)[None, :],
            lengths[None, :],
            0,
        ),
        axis=1,
        dtype=jnp.int32,
    )
    seg_ends = jnp.cumsum(picked, dtype=jnp.int32)
    places = jnp.arange(win_rows, dtype=jnp.int32)
    return jnp.sum(
        jnp.where(seg_ends[None, :] <= places[:, None], picked[None, :], 0), axis=1, dtype=jnp.int32
    )


def local(queries, rotated_key_matrix, value_matrix, out_weight, out_grad, lengths, pack_order):
    seq_count = lax.psum(1, SEQ)
    x_count = lax.psum(1, "x")
    core_count = lax.psum(1, "core")
    tok = queries.shape[1]
    head_scale = HEAD_SIZE ** (-0.5)
    hq = QUERY_HEADS // seq_count
    hk = KEY_VALUE_HEADS // seq_count
    group_width = hq // hk
    packed = jnp.concatenate(
        [
            queries.reshape(tok, seq_count, hq, HEAD_SIZE),
            rotated_key_matrix.reshape(tok, seq_count, hk, HEAD_SIZE),
            value_matrix.reshape(tok, seq_count, hk, HEAD_SIZE),
        ],
        axis=2,
    ).transpose(1, 0, 2, 3)
    got = lax.all_to_all(packed, SEQ, split_axis=0, concat_axis=0, tiled=True)
    win_rows = seq_count * tok
    got = got.reshape(win_rows, hq + 2 * hk, HEAD_SIZE)
    query_head_rows = got[:, :hq].reshape(win_rows, hk, group_width, HEAD_SIZE)
    k_loc = got[:, hq : hq + hk]
    v_loc = got[:, hq + hk :]
    starts = row_starts(lengths[0], pack_order[0], win_rows)
    blk = min(BLOCK, win_rows)
    blk_count = win_rows // blk
    reach = -(-(MOST - 1) // blk)

    def band(i):
        q_start = i * blk
        k_start = max(0, q_start - reach * blk)
        return q_start, k_start, q_start + blk

    def probs(i, q_blk, m=None, l=None):
        q_start, k_start, k_end = band(i)
        k_band = k_loc[k_start:k_end]
        scores = (
            jnp.einsum("qkgd,skd->kgqs", q_blk, k_band, preferred_element_type=jnp.float32)
            * head_scale
        )
        rows_at = q_start + jnp.arange(blk, dtype=jnp.int32)
        cols_at = k_start + jnp.arange(k_end - k_start, dtype=jnp.int32)
        first_at = starts[q_start : q_start + blk]
        visible = (cols_at[None, :] >= first_at[:, None]) & (cols_at[None, :] <= rows_at[:, None])
        if m is None:
            m = jnp.max(jnp.where(visible, scores, -1e30), axis=-1, keepdims=True)
        expd = jnp.where(visible, jnp.exp(scores - m), 0.0)
        if l is None:
            l = jnp.sum(expd, axis=-1, keepdims=True)
        return expd / l, m, l

    out_blocks, stats = [], []
    for i in range(blk_count):
        q_start, k_start, k_end = band(i)
        q_blk = query_head_rows[q_start : q_start + blk]
        attn_prob, m, l = probs(i, q_blk)
        stats.append((m, l))
        out_blocks.append(
            jnp.einsum(
                "kgqs,skd->qkgd",
                attn_prob.astype(jnp.bfloat16),
                v_loc[k_start:k_end],
                preferred_element_type=jnp.float32,
            ).astype(jnp.bfloat16)
        )
    attn_out = jnp.concatenate(out_blocks, axis=0)
    a_head = attn_out.reshape(win_rows, hq * HEAD_SIZE)
    product = jnp.dot(a_head, out_weight, preferred_element_type=jnp.float32)
    pieces = (
        product.astype(jnp.bfloat16)
        .reshape(x_count, core_count, tok, product.shape[1])
        .transpose(1, 0, 2, 3)
    )
    incoming = lax.all_gather(out_grad.reshape(tok, out_grad.shape[2]), SEQ, axis=0, tiled=True)
    wo_grad = lax.dot_general(
        a_head, incoming, (((0,), (0,)), ((), ())), preferred_element_type=jnp.float32
    )
    d_rows = lax.dot_general(
        incoming, out_weight, (((1,), (1,)), ((), ())), preferred_element_type=jnp.float32
    )
    attention_grad = d_rows.astype(jnp.bfloat16).reshape(win_rows, hk, group_width, HEAD_SIZE)
    pieces, attention_grad = lax.optimization_barrier((pieces, attention_grad))
    core_at = lax.axis_index("core")
    kept = lax.dynamic_index_in_dim(pieces, core_at, axis=0, keepdims=False)
    sent = lax.dynamic_index_in_dim(pieces, 1 - core_at, axis=0, keepdims=False)
    sent = lax.ppermute(sent, "core", perm=[(0, 1), (1, 0)])
    pieces = (kept.astype(jnp.float32) + sent.astype(jnp.float32)).astype(jnp.bfloat16)
    pieces = lax.all_to_all(pieces, "x", split_axis=0, concat_axis=0, tiled=True)

    dq_blocks = []
    dk_blocks = [None] * blk_count
    dv_blocks = [None] * blk_count
    for i in range(blk_count):
        if i == blk_count - 1:
            pieces, attention_grad = lax.optimization_barrier((pieces, attention_grad))
        q_start, k_start, k_end = band(i)
        q_blk = query_head_rows[q_start : q_start + blk]
        g_blk = attention_grad[q_start : q_start + blk]
        o_blk = attn_out[q_start : q_start + blk]
        row_dot = jnp.sum(g_blk.astype(jnp.float32) * o_blk.astype(jnp.float32), axis=-1)
        row_dot = jnp.transpose(row_dot, (1, 2, 0))[..., None]
        attn_prob, _, _ = probs(i, q_blk, *stats[i])
        k_band = k_loc[k_start:k_end]
        v_band = v_loc[k_start:k_end]
        d_prob = jnp.einsum("qkgd,skd->kgqs", g_blk, v_band, preferred_element_type=jnp.float32)
        score_gradient = (attn_prob * (d_prob - row_dot) * head_scale).astype(jnp.bfloat16)
        dq_blocks.append(
            jnp.einsum(
                "kgqs,skd->qkgd", score_gradient, k_band, preferred_element_type=jnp.float32
            ).astype(jnp.bfloat16)
        )
        dk_part = jnp.einsum(
            "kgqs,qkgd->skd", score_gradient, q_blk, preferred_element_type=jnp.float32
        )
        dv_part = jnp.einsum(
            "kgqs,qkgd->skd",
            attn_prob.astype(jnp.bfloat16),
            g_blk,
            preferred_element_type=jnp.float32,
        )
        for j in range(k_start // blk, k_end // blk):
            lo = j * blk - k_start
            for acc, part in ((dk_blocks, dk_part), (dv_blocks, dv_part)):
                piece = part[lo : lo + blk]
                acc[j] = piece if acc[j] is None else acc[j] + piece
    y_out = jnp.sum(pieces.astype(jnp.float32), axis=0).astype(jnp.bfloat16)
    dq_all = jnp.concatenate(dq_blocks, axis=0).reshape(win_rows, hq, HEAD_SIZE)
    dk_all = jnp.concatenate(dk_blocks, axis=0).astype(jnp.bfloat16)
    dv_all = jnp.concatenate(dv_blocks, axis=0).astype(jnp.bfloat16)
    packed_out = jnp.concatenate([dq_all, dk_all, dv_all], axis=1).reshape(
        seq_count, tok, hq + 2 * hk, HEAD_SIZE
    )
    back = lax.all_to_all(packed_out, SEQ, split_axis=0, concat_axis=0, tiled=True)
    back = back.transpose(1, 0, 2, 3)
    d_q = back[:, :, :hq].reshape(1, tok, QUERY_HEADS * HEAD_SIZE)
    key_gradient = back[:, :, hq : hq + hk].reshape(1, tok, KEY_VALUE_HEADS * HEAD_SIZE)
    value_gradient = back[:, :, hq + hk :].reshape(1, tok, KEY_VALUE_HEADS * HEAD_SIZE)
    y_count = lax.psum(1, "dpy")
    z_count = lax.psum(1, "dpz")
    cols = wo_grad.shape[1]
    wo_perm = (
        wo_grad.reshape(wo_grad.shape[0], y_count, z_count, cols // (y_count * z_count))
        .transpose(0, 2, 1, 3)
        .reshape(wo_grad.shape[0], cols)
    )
    wo_perm = lax.psum_scatter(wo_perm, "dpz", scatter_dimension=1, tiled=True)
    weight_grad = lax.psum_scatter(wo_perm, "dpy", scatter_dimension=1, tiled=True)
    return (
        y_out.reshape(1, tok, y_out.shape[1]),
        d_q,
        key_gradient,
        value_gradient,
        weight_grad,
    )


def solution(mesh):
    dp_count = mesh.shape["dp"]
    y_count = 4 if dp_count % 4 == 0 else 1
    seq_count = mesh.shape["seq"]
    core_count = 2 if seq_count % 2 == 0 else 1
    mesh = Mesh(
        mesh.devices.reshape(
            seq_count // core_count, core_count, y_count, dp_count // y_count
        ),
        ("x", "core", "dpy", "dpz"),
    )
    in_specs = (
        P(DP, SEQ, None),
        P(DP, SEQ, None),
        P(DP, SEQ, None),
        P(SEQ, None),
        P(DP, SEQ, None),
        P(DP, None),
        P(DP, None),
    )
    out_specs = (
        P(DP, SEQ, None),
        P(DP, SEQ, None),
        P(DP, SEQ, None),
        P(DP, SEQ, None),
        P(SEQ, DP),
    )
    return jax.shard_map(local, mesh=mesh, in_specs=in_specs, out_specs=out_specs, check_vma=False)
```
